128 devices in a mesh: dp: 8 (over x, core), fsdp: 16 (over y, z).
Axes of the slice: x: 4, y: 4, z: 4, core: 2. Of those that a mesh axis runs over, the one named last changes fastest.
Arguments:
- tokens: bfloat16 [65536, 8192], P(('dp', 'fsdp')), may hold values from -6 to 6
- frozen_value_matrix: bfloat16 [8192, 1024], P('fsdp'), may hold values from -0.0625 to 0.0625
- adapter_down_maps: bfloat16 [512, 64, 8192], P('dp', None, 'fsdp'), may hold values from -0.0625 to 0.0625
- adapter_up_maps: bfloat16 [512, 64, 1024], P('dp', None, 'fsdp'), may hold values from -0.375 to 0.375
- value_output_gradient: bfloat16 [65536, 1024], P(('dp', 'fsdp')), may hold values from -0.125 to 0.125
- window_composer_position: int32 [8, 64], P('dp'), may hold values from 0 to 3
- needed_composers: int32 [8, 4], replicated, may hold values from 0 to 511, as said below
- composer_storage_index: int32 [512], replicated, may hold values from 0 to 511, as said below
Outputs:
- value: bfloat16 [65536, 1024], P(('dp', 'fsdp'))
- grad_down: float32 [512, 64, 8192], P('dp', None, 'fsdp')
- grad_up: float32 [512, 64, 1024], P('dp', None, 'fsdp')
The draws below stay inside these ranges and needn't reach their ends.
Inputs may be any that keep to these rules, and one draw needn't show every extreme that they name: Every storage index appears once: the adapters and gradients of composer c lie at index composer_storage_index[c]; composer c is owned by index composer_storage_index[c] // 64 of dp. `needed_composers`: the 4 composers of one row have 4 different owners along dp.
All inputs are finite; a program needn't handle non-finite values.
Results may differ from the reference program's by a relative error of at most 0.004.
Values may be sent and summed in bfloat16 or wider, within the bound.
No kernel may reach another device: no remote copies, remote signals or barrier semaphores. Data moves between devices by JAX's collectives and lax.ppermute only.
A program may use at most 128 MiB of HBM per device.

```python
import jax
import jax.numpy as jnp
from jax import lax

MODEL_WIDTH = 8192
ADAPTER_RANK = 64
CPD = 64
GNEED = 4
WIN = 128
VALUE_FEATURES = 1024
COMPOSER_COUNT = 512
GROUPS = 8
SEQ_DEV = 4
TOKENS = 65536
N_DP = 8
N_FSDP = 16


def composer_tables(key):
    placed = jax.random.permutation(jax.random.fold_in(key, 11), COMPOSER_COUNT).astype(jnp.int32)
    inverse = jnp.argsort(placed, stable=True).astype(jnp.int32)
    owner_keys = jax.random.split(jax.random.fold_in(key, 12), GROUPS)
    owners = jax.vmap(lambda sub: jax.random.permutation(sub, GROUPS)[:GNEED])(owner_keys).astype(jnp.int32)
    first = jax.random.randint(jax.random.fold_in(key, 13), (GROUPS, GNEED), 0, CPD)
    second = jax.random.randint(jax.random.fold_in(key, 14), (GROUPS, GNEED), 0, CPD)
    local_index = jnp.minimum(first, second).astype(jnp.int32)
    storage_indices = owners * CPD + local_index
    needed = inverse[storage_indices]
    return (placed, needed.astype(jnp.int32))


def draw_composer_storage_index(key, part):
    return composer_tables(key)[0]


def draw_needed_composers(key, part):
    return composer_tables(key)[1]


def with_ends(result, rng, least, high):
    extent = result.shape
    place = [jax.random.randint(jax.random.fold_in(rng, axis), (), 0, extent[axis]) for axis in range(len(extent))]
    result = result.at[tuple(place)].set(least)
    longest = extent.index(max(extent))
    place[longest] = (place[longest] + 1) % extent[longest]
    return result.at[tuple(place)].set(high)


def shard_levels(own_key, extent, cuts, smallest, top_value):
    factor_of, own = 1.0, jax.random.fold_in(own_key, 6)
    for axis_at, blocks in cuts:
        heights = jnp.exp(jax.random.uniform(jax.random.fold_in(own, axis_at), (blocks,), jnp.float32, smallest / len(cuts), top_value / len(cuts)))
        factor_of = factor_of * jnp.repeat(heights, extent[axis_at] // blocks).reshape([-1 if axis == axis_at else 1 for axis in range(len(extent))])
    return factor_of


def gaussian(key, dims, width, most, cuts=(), held_as=jnp.bfloat16):
    array = width * jax.random.normal(key, dims, jnp.float32)
    if cuts:
        array = array * shard_levels(key, dims, cuts, -0.22, 0.18)
    return jnp.clip(array, -most, most).astype(held_as)


def setup_inputs(seed: int = 0) -> dict:
    splits = jax.random.split(jax.random.key(seed), 9)
    tokens = gaussian(splits[0], (TOKENS, MODEL_WIDTH), 1.0, 6.0, ((0, 128),))
    frozen_value_matrix = gaussian(splits[1], (MODEL_WIDTH, VALUE_FEATURES), MODEL_WIDTH ** -0.5, 0.0625, ((0, 16),))
    adapter_down_maps = gaussian(splits[2], (COMPOSER_COUNT, ADAPTER_RANK, MODEL_WIDTH), MODEL_WIDTH ** -0.5, 0.0625, ((0, 8), (2, 16)))
    adapter_up_maps = gaussian(splits[3], (COMPOSER_COUNT, ADAPTER_RANK, VALUE_FEATURES), (4 * ADAPTER_RANK) ** -0.5, 0.375, ((0, 8), (2, 16)))
    value_output_gradient = gaussian(splits[4], (TOKENS, VALUE_FEATURES), 0.02, 0.125, ((0, 128),))
    window_composer_position = with_ends(jax.random.randint(splits[5], (GROUPS, N_FSDP * SEQ_DEV), 0, GNEED), jax.random.fold_in(splits[5], 1), 0, GNEED - 1).astype(jnp.int32)
    needed_composers = draw_needed_composers(jax.random.fold_in(splits[8], 71), 0)
    composer_storage_index = draw_composer_storage_index(jax.random.fold_in(splits[8], 71), 0)
    return {"tokens": tokens, "frozen_value_matrix": frozen_value_matrix, "adapter_down_maps": adapter_down_maps, "adapter_up_maps": adapter_up_maps, "value_output_gradient": value_output_gradient, "window_composer_position": window_composer_position, "needed_composers": needed_composers, "composer_storage_index": composer_storage_index}


ADAPTER_SCALE = 2.0


def reference(tokens, frozen_value_matrix, adapter_down_maps, adapter_up_maps, value_output_gradient, window_composer_position, needed_composers, composer_storage_index):
    group_win = N_FSDP * SEQ_DEV
    slots_all = composer_storage_index[needed_composers].astype(jnp.int32)
    x_all = tokens.reshape(N_DP, group_win, WIN, MODEL_WIDTH)
    dv_all = value_output_gradient.reshape(N_DP, group_win, WIN, VALUE_FEATURES)
    slot_range = jnp.arange(GNEED, dtype=jnp.int32)

    def step(carry, items):
        grad_down, grad_up = carry
        x_grp, value_gradient_group, picks, storage_indices = items
        down_matrix = adapter_down_maps[storage_indices].astype(jnp.float32)
        upward_matrix = adapter_up_maps[storage_indices].astype(jnp.float32)
        hot = (picks[:, None] == slot_range[None, :]).astype(jnp.float32)
        down_w = jnp.einsum("wk,krd->wrd", hot, down_matrix)
        up_weight = jnp.einsum("wk,krc->wrc", hot, upward_matrix)
        xf = x_grp.astype(jnp.float32)
        frozen_rows = jnp.dot(x_grp.reshape(-1, MODEL_WIDTH), frozen_value_matrix, preferred_element_type=jnp.float32)
        low = jnp.einsum("wtd,wrd->wtr", xf, down_w).astype(jnp.bfloat16)
        rank_projected_float = low.astype(jnp.float32)
        adapter_change = jnp.einsum("wtr,wrc->wtc", rank_projected_float, up_weight).reshape(-1, VALUE_FEATURES)
        value = (frozen_rows + ADAPTER_SCALE * adapter_change).astype(jnp.bfloat16)
        value_gradient_float = value_gradient_group.astype(jnp.float32)
        backward_rows = (ADAPTER_SCALE * jnp.einsum("bdu,bku->bdk", value_gradient_float, up_weight)).astype(jnp.bfloat16).astype(jnp.float32)
        per_down = jnp.einsum("wtr,wtd->wrd", backward_rows, xf)
        part_down = jnp.einsum("wk,wrd->krd", hot, per_down)
        each_up_matrix = jnp.einsum("noy,nod->nyd", ADAPTER_SCALE * rank_projected_float, value_gradient_float)
        part_up = jnp.einsum("wk,wrc->krc", hot, each_up_matrix)
        grad_down = grad_down.at[storage_indices].add(part_down)
        grad_up = grad_up.at[storage_indices].add(part_up)
        return (grad_down, grad_up), value

    init = (jnp.zeros((COMPOSER_COUNT, ADAPTER_RANK, MODEL_WIDTH), jnp.float32), jnp.zeros((COMPOSER_COUNT, ADAPTER_RANK, VALUE_FEATURES), jnp.float32))
    (grad_down, grad_up), values = lax.scan(step, init, (x_all, dv_all, window_composer_position, slots_all))
    return values.reshape(TOKENS, VALUE_FEATURES), grad_down, grad_up
```

```python
import jax
import jax.numpy as jnp
from jax import lax
from jax.sharding import PartitionSpec as P

WIN = 128


ADAPTER_SCALE = 2.0


def body(
    tokens,
    frozen_value_matrix,
    adapter_down_maps,
    adapter_up_maps,
    value_output_gradient,
    window_composer_position,
    needed_composers,
    composer_storage_index,
):
    f32, bf16 = jnp.float32, jnp.bfloat16
    dp_count = lax.axis_size("dp")
    fsdp_count = lax.axis_size("fsdp")
    group_index = lax.axis_index("dp")
    member_index = lax.axis_index("fsdp")
    tok_rows, width = tokens.shape
    value_cols = frozen_value_matrix.shape[1]
    rank = adapter_down_maps.shape[1]
    each_owner_rows = adapter_down_maps.shape[0]
    down_cols = adapter_down_maps.shape[2]
    up_cols = adapter_up_maps.shape[2]
    list_len = needed_composers.shape[1]
    windows = tok_rows // WIN

    core = group_index % 2
    half = value_cols // 2
    w_mine = lax.dynamic_slice_in_dim(frozen_value_matrix, core * half, half, axis=1)
    w_mine_full = lax.all_gather(w_mine, "fsdp", axis=0, tiled=True)
    w_other_full = lax.ppermute(w_mine_full, "dp", [(i, i ^ 1) for i in range(dp_count)])
    out_mine = jnp.dot(tokens, w_mine_full, preferred_element_type=f32)
    out_other = jnp.dot(tokens, w_other_full, preferred_element_type=f32)
    frozen_rows = jnp.where(
        core == 0,
        jnp.concatenate([out_mine, out_other], axis=1),
        jnp.concatenate([out_other, out_mine], axis=1),
    )

    list_slot = jnp.take(composer_storage_index, needed_composers, axis=0)
    list_owner = list_slot // each_owner_rows
    list_local = list_slot % each_owner_rows
    owned_here = list_owner == group_index
    locally_owned_slots = jnp.sum(jnp.where(owned_here, list_local, 0), axis=1)
    owned_any = jnp.any(owned_here, axis=1)
    send = jnp.concatenate(
        [
            jnp.take(adapter_down_maps, locally_owned_slots, axis=0),
            jnp.take(adapter_up_maps, locally_owned_slots, axis=0),
        ],
        axis=2,
    )
    send = jnp.where(owned_any[:, None, None], send, jnp.zeros((), send.dtype))
    got = lax.all_to_all(send, "dp", split_axis=0, concat_axis=0, tiled=True)
    my_owner = lax.dynamic_index_in_dim(list_owner, group_index, 0, keepdims=False)
    slab = jnp.take(got, my_owner, axis=0)
    shares = lax.all_gather(slab, "fsdp", axis=0, tiled=False)
    full_down = shares[..., :down_cols].transpose(1, 2, 0, 3).reshape(list_len, rank, width)
    full_up = shares[..., down_cols:].transpose(1, 2, 0, 3).reshape(list_len, rank, value_cols)

    group_picks = window_composer_position[0]
    my_picks = lax.dynamic_slice_in_dim(group_picks, member_index * windows, windows, 0)
    slot_range = jnp.arange(list_len, dtype=jnp.int32)
    token_hot = jnp.broadcast_to(
        my_picks[:, None, None] == slot_range[None, None, :], (windows, WIN, list_len)
    ).reshape(tok_rows, list_len)
    hot_f = token_hot.astype(f32)

    down_flat = full_down.reshape(list_len * rank, width)
    up_flat = full_up.reshape(list_len * rank, value_cols)
    low_all = lax.dot_general(
        tokens, down_flat, (((1,), (1,)), ((), ())), preferred_element_type=f32
    ).reshape(tok_rows, list_len, rank)
    low = jnp.sum(low_all * hot_f[:, :, None], axis=1).astype(bf16)
    hot_h = token_hot.astype(bf16)
    masked_low = (hot_h[:, :, None] * low[:, None, :]).reshape(tok_rows, list_len * rank)
    adapter_change = jnp.dot(masked_low, up_flat, preferred_element_type=f32)
    value = (frozen_rows + ADAPTER_SCALE * adapter_change).astype(bf16)

    back_all = lax.dot_general(
        value_output_gradient, up_flat, (((1,), (1,)), ((), ())), preferred_element_type=f32
    ).reshape(tok_rows, list_len, rank)
    back = (ADAPTER_SCALE * jnp.sum(back_all * hot_f[:, :, None], axis=1)).astype(bf16)
    masked_back = (hot_h[:, :, None] * back[:, None, :]).reshape(tok_rows, list_len * rank)
    scaled_masked_low = masked_low * jnp.asarray(ADAPTER_SCALE, bf16)

    contract = (((0,), (0,)), ((), ()))
    part_down = lax.dot_general(masked_back, tokens, contract, preferred_element_type=f32)
    part_up = lax.dot_general(
        scaled_masked_low, value_output_gradient, contract, preferred_element_type=f32
    )
    rows = list_len * rank
    part_down = part_down.reshape(rows, fsdp_count, down_cols).transpose(1, 0, 2)
    part_up = part_up.reshape(rows, fsdp_count, up_cols).transpose(1, 0, 2)
    summed = lax.psum_scatter(
        jnp.concatenate([part_down, part_up], axis=2), "fsdp", scatter_dimension=0, tiled=True
    )[0]

    owner_range = jnp.arange(dp_count, dtype=jnp.int32)
    to_owner = my_owner[None, :] == owner_range[:, None]
    pick_index = jnp.sum(jnp.where(to_owner, slot_range[None, :], 0), axis=1)
    owner_has = jnp.any(to_owner, axis=1)
    send_grad = jnp.take(summed.reshape(list_len, rank, down_cols + up_cols), pick_index, axis=0)
    send_grad = jnp.where(owner_has[:, None, None], send_grad, 0.0)
    back_grad = lax.all_to_all(send_grad, "dp", split_axis=0, concat_axis=0, tiled=True)
    local_range = jnp.arange(each_owner_rows, dtype=jnp.int32)
    arrivals = owned_any[:, None] & (locally_owned_slots[:, None] == local_range[None, :])
    arrive_f = arrivals.astype(f32)
    grad_down = jnp.sum(
        arrive_f[:, :, None, None] * back_grad[:, None, :, :down_cols], axis=0
    )
    grad_up = jnp.sum(arrive_f[:, :, None, None] * back_grad[:, None, :, down_cols:], axis=0)
    return (value, grad_down, grad_up)


def solution(mesh):
    return jax.shard_map(
        body,
        mesh=mesh,
        in_specs=(
            P(("dp", "fsdp"), None),
            P("fsdp", None),
            P("dp", None, "fsdp"),
            P("dp", None, "fsdp"),
            P(("dp", "fsdp"), None),
            P("dp", None),
            P(),
            P(),
        ),
        out_specs=(P(("dp", "fsdp"), None), P("dp", None, "fsdp"), P("dp", None, "fsdp")),
        check_vma=False,
    )
```

```python
import jax
import jax.numpy as jnp
from jax import lax
from jax.sharding import PartitionSpec as P

WIN = 128


ADAPTER_SCALE = 2.0


def body(
    tokens,
    frozen_value_matrix,
    adapter_down_maps,
    adapter_up_maps,
    value_output_gradient,
    window_composer_position,
    needed_composers,
    composer_storage_index,
):
    f32, bf16 = jnp.float32, jnp.bfloat16
    dp_count = lax.axis_size("dp")
    fsdp_count = lax.axis_size("fsdp")
    group_index = lax.axis_index("dp")
    member_index = lax.axis_index("fsdp")
    tok_rows, width = tokens.shape
    value_cols = frozen_value_matrix.shape[1]
    rank = adapter_down_maps.shape[1]
    each_owner_rows = adapter_down_maps.shape[0]
    down_cols = adapter_down_maps.shape[2]
    up_cols = adapter_up_maps.shape[2]
    list_len = needed_composers.shape[1]
    windows = tok_rows // WIN

    part_cols = value_cols // dp_count
    w_part = lax.dynamic_slice_in_dim(
        frozen_value_matrix, group_index * part_cols, part_cols, axis=1
    )
    w_part_full = lax.all_gather(w_part, "fsdp", axis=0, tiled=True)
    same_parity = [w_part_full]
    for step in range(1, dp_count // 2):
        same_parity.append(
            lax.ppermute(
                w_part_full, "dp", [(i, (i + 2 * step) % dp_count) for i in range(dp_count)]
            )
        )
    w_own = jnp.concatenate(same_parity, axis=1)
    w_partner = lax.ppermute(w_own, "dp", [(i, i ^ 1) for i in range(dp_count)])
    out_own = jnp.dot(tokens, w_own, preferred_element_type=f32)
    out_partner = jnp.dot(tokens, w_partner, preferred_element_type=f32)
    held = jnp.concatenate([out_own, out_partner], axis=1).reshape(tok_rows, dp_count, part_cols)
    part_ids = jnp.arange(dp_count, dtype=jnp.int32)
    partner_index = group_index ^ 1
    same = (part_ids % 2) == (group_index % 2)
    where_held = jnp.where(
        same,
        ((group_index - part_ids) % dp_count) // 2,
        dp_count // 2 + ((partner_index - part_ids) % dp_count) // 2,
    )
    frozen_rows = jnp.take(held, where_held, axis=1).reshape(tok_rows, value_cols)

    list_slot = jnp.take(composer_storage_index, needed_composers, axis=0)
    list_owner = list_slot // each_owner_rows
    list_local = list_slot % each_owner_rows
    owned_here = list_owner == group_index
    locally_owned_slots = jnp.sum(jnp.where(owned_here, list_local, 0), axis=1)
    owned_any = jnp.any(owned_here, axis=1)
    send = jnp.concatenate(
        [
            jnp.take(adapter_down_maps, locally_owned_slots, axis=0),
            jnp.take(adapter_up_maps, locally_owned_slots, axis=0),
        ],
        axis=2,
    )
    send = jnp.where(owned_any[:, None, None], send, jnp.zeros((), send.dtype))
    got = lax.all_to_all(send, "dp", split_axis=0, concat_axis=0, tiled=True)
    my_owner = lax.dynamic_index_in_dim(list_owner, group_index, 0, keepdims=False)
    slab = jnp.take(got, my_owner, axis=0)
    shares = lax.all_gather(slab, "fsdp", axis=0, tiled=False)
    full_down = shares[..., :down_cols].transpose(1, 2, 0, 3).reshape(list_len, rank, width)
    full_up = shares[..., down_cols:].transpose(1, 2, 0, 3).reshape(list_len, rank, value_cols)

    group_picks = window_composer_position[0]
    my_picks = lax.dynamic_slice_in_dim(group_picks, member_index * windows, windows, 0)
    slot_range = jnp.arange(list_len, dtype=jnp.int32)
    token_hot = jnp.broadcast_to(
        my_picks[:, None, None] == slot_range[None, None, :], (windows, WIN, list_len)
    ).reshape(tok_rows, list_len)
    hot_f = token_hot.astype(f32)

    down_flat = full_down.reshape(list_len * rank, width)
    up_flat = full_up.reshape(list_len * rank, value_cols)
    low_all = lax.dot_general(
        tokens, down_flat, (((1,), (1,)), ((), ())), preferred_element_type=f32
    ).reshape(tok_rows, list_len, rank)
    low = jnp.sum(low_all * hot_f[:, :, None], axis=1).astype(bf16)
    hot_h = token_hot.astype(bf16)
    masked_low = (hot_h[:, :, None] * low[:, None, :]).reshape(tok_rows, list_len * rank)
    adapter_change = jnp.dot(masked_low, up_flat, preferred_element_type=f32)
    value = (frozen_rows + ADAPTER_SCALE * adapter_change).astype(bf16)

    back_all = lax.dot_general(
        value_output_gradient, up_flat, (((1,), (1,)), ((), ())), preferred_element_type=f32
    ).reshape(tok_rows, list_len, rank)
    back = (ADAPTER_SCALE * jnp.sum(back_all * hot_f[:, :, None], axis=1)).astype(bf16)
    masked_back = (hot_h[:, :, None] * back[:, None, :]).reshape(tok_rows, list_len * rank)
    scaled_masked_low = masked_low * jnp.asarray(ADAPTER_SCALE, bf16)

    contract = (((0,), (0,)), ((), ()))
    part_down = lax.dot_general(masked_back, tokens, contract, preferred_element_type=f32)
    part_up = lax.dot_general(
        scaled_masked_low, value_output_gradient, contract, preferred_element_type=f32
    )
    rows = list_len * rank
    part_down = part_down.reshape(rows, fsdp_count, down_cols).transpose(1, 0, 2)
    part_up = part_up.reshape(rows, fsdp_count, up_cols).transpose(1, 0, 2)
    summed = lax.psum_scatter(
        jnp.concatenate([part_down, part_up], axis=2), "fsdp", scatter_dimension=0, tiled=True
    )[0]

    owner_range = jnp.arange(dp_count, dtype=jnp.int32)
    to_owner = my_owner[None, :] == owner_range[:, None]
    pick_index = jnp.sum(jnp.where(to_owner, slot_range[None, :], 0), axis=1)
    owner_has = jnp.any(to_owner, axis=1)
    send_grad = jnp.take(summed.reshape(list_len, rank, down_cols + up_cols), pick_index, axis=0)
    send_grad = jnp.where(owner_has[:, None, None], send_grad, 0.0)
    back_grad = lax.all_to_all(send_grad, "dp", split_axis=0, concat_axis=0, tiled=True)
    land = jnp.where(owned_any, locally_owned_slots, 0)
    arrived = jnp.where(owned_any[:, None, None], back_grad, 0.0)
    grad_down = jnp.zeros((each_owner_rows, rank, down_cols), f32).at[land].add(
        arrived[:, :, :down_cols]
    )
    grad_up = jnp.zeros((each_owner_rows, rank, up_cols), f32).at[land].add(
        arrived[:, :, down_cols:]
    )
    return (value, grad_down, grad_up)


def solution(mesh):
    return jax.shard_map(
        body,
        mesh=mesh,
        in_specs=(
            P(("dp", "fsdp"), None),
            P("fsdp", None),
            P("dp", None, "fsdp"),
            P("dp", None, "fsdp"),
            P(("dp", "fsdp"), None),
            P("dp", None),
            P(),
            P(),
        ),
        out_specs=(P(("dp", "fsdp"), None), P("dp", None, "fsdp"), P("dp", None, "fsdp")),
        check_vma=False,
    )
```

```python
import jax
import jax.numpy as jnp
from jax import lax
from jax.sharding import PartitionSpec as P

WIN = 128


ADAPTER_SCALE = 2.0


def body(
    tokens,
    frozen_value_matrix,
    adapter_down_maps,
    adapter_up_maps,
    value_output_gradient,
    window_composer_position,
    needed_composers,
    composer_storage_index,
):
    f32, bf16 = jnp.float32, jnp.bfloat16
    dp_count = lax.axis_size("dp")
    fsdp_count = lax.axis_size("fsdp")
    group_index = lax.axis_index("dp")
    member_index = lax.axis_index("fsdp")
    tok_rows, width = tokens.shape
    value_cols = frozen_value_matrix.shape[1]
    rank = adapter_down_maps.shape[1]
    each_owner_rows = adapter_down_maps.shape[0]
    down_cols = adapter_down_maps.shape[2]
    up_cols = adapter_up_maps.shape[2]
    list_len = needed_composers.shape[1]
    windows = tok_rows // WIN

    part_cols = value_cols // dp_count
    w_part = lax.dynamic_slice_in_dim(
        frozen_value_matrix, group_index * part_cols, part_cols, axis=1
    )
    w_part_full = lax.all_gather(w_part, "fsdp", axis=0, tiled=True)
    up_x = [(i, (i + 2) % dp_count) for i in range(dp_count)]
    down_x = [(i, (i - 2) % dp_count) for i in range(dp_count)]
    from_left = lax.ppermute(w_part_full, "dp", up_x)
    from_right = lax.ppermute(w_part_full, "dp", down_x)
    half_part = part_cols // 2
    far_a = lax.ppermute(from_left[:, :half_part], "dp", up_x)
    far_b = lax.ppermute(from_right[:, half_part:], "dp", down_x)
    far = jnp.concatenate([far_a, far_b], axis=1)
    same_parity = [w_part_full, from_left, far, from_right]
    w_own = jnp.concatenate(same_parity, axis=1)
    w_partner = lax.ppermute(w_own, "dp", [(i, i ^ 1) for i in range(dp_count)])
    out_own = jnp.dot(tokens, w_own, preferred_element_type=f32)
    out_partner = jnp.dot(tokens, w_partner, preferred_element_type=f32)
    held = jnp.concatenate([out_own, out_partner], axis=1).reshape(tok_rows, dp_count, part_cols)
    part_ids = jnp.arange(dp_count, dtype=jnp.int32)
    partner_index = group_index ^ 1
    same = (part_ids % 2) == (group_index % 2)
    where_held = jnp.where(
        same,
        ((group_index - part_ids) % dp_count) // 2,
        dp_count // 2 + ((partner_index - part_ids) % dp_count) // 2,
    )
    frozen_rows = jnp.take(held, where_held, axis=1).reshape(tok_rows, value_cols)

    list_slot = jnp.take(composer_storage_index, needed_composers, axis=0)
    list_owner = list_slot // each_owner_rows
    list_local = list_slot % each_owner_rows
    owned_here = list_owner == group_index
    locally_owned_slots = jnp.sum(jnp.where(owned_here, list_local, 0), axis=1)
    owned_any = jnp.any(owned_here, axis=1)
    send = jnp.concatenate(
        [
            jnp.take(adapter_down_maps, locally_owned_slots, axis=0),
            jnp.take(adapter_up_maps, locally_owned_slots, axis=0),
        ],
        axis=2,
    )
    send = jnp.where(owned_any[:, None, None], send, jnp.zeros((), send.dtype))
    got = lax.all_to_all(send, "dp", split_axis=0, concat_axis=0, tiled=True)
    my_owner = lax.dynamic_index_in_dim(list_owner, group_index, 0, keepdims=False)
    slab = jnp.take(got, my_owner, axis=0)
    shares = lax.all_gather(slab, "fsdp", axis=0, tiled=False)
    full_down = shares[..., :down_cols].transpose(1, 2, 0, 3).reshape(list_len, rank, width)
    full_up = shares[..., down_cols:].transpose(1, 2, 0, 3).reshape(list_len, rank, value_cols)

    group_picks = window_composer_position[0]
    my_picks = lax.dynamic_slice_in_dim(group_picks, member_index * windows, windows, 0)
    slot_range = jnp.arange(list_len, dtype=jnp.int32)
    token_hot = jnp.broadcast_to(
        my_picks[:, None, None] == slot_range[None, None, :], (windows, WIN, list_len)
    ).reshape(tok_rows, list_len)
    hot_f = token_hot.astype(f32)

    down_flat = full_down.reshape(list_len * rank, width)
    up_flat = full_up.reshape(list_len * rank, value_cols)
    low_all = lax.dot_general(
        tokens, down_flat, (((1,), (1,)), ((), ())), preferred_element_type=f32
    ).reshape(tok_rows, list_len, rank)
    low = jnp.sum(low_all * hot_f[:, :, None], axis=1).astype(bf16)
    hot_h = token_hot.astype(bf16)
    masked_low = (hot_h[:, :, None] * low[:, None, :]).reshape(tok_rows, list_len * rank)
    adapter_change = jnp.dot(masked_low, up_flat, preferred_element_type=f32)
    value = (frozen_rows + ADAPTER_SCALE * adapter_change).astype(bf16)

    back_all = lax.dot_general(
        value_output_gradient, up_flat, (((1,), (1,)), ((), ())), preferred_element_type=f32
    ).reshape(tok_rows, list_len, rank)
    back = (ADAPTER_SCALE * jnp.sum(back_all * hot_f[:, :, None], axis=1)).astype(bf16)
    masked_back = (hot_h[:, :, None] * back[:, None, :]).reshape(tok_rows, list_len * rank)
    scaled_masked_low = masked_low * jnp.asarray(ADAPTER_SCALE, bf16)

    contract = (((0,), (0,)), ((), ()))
    part_down = lax.dot_general(masked_back, tokens, contract, preferred_element_type=f32)
    part_up = lax.dot_general(
        scaled_masked_low, value_output_gradient, contract, preferred_element_type=f32
    )
    rows = list_len * rank
    part_down = part_down.reshape(rows, fsdp_count, down_cols).transpose(1, 0, 2)
    part_up = part_up.reshape(rows, fsdp_count, up_cols).transpose(1, 0, 2)
    sum_down = lax.psum_scatter(part_down, "fsdp", scatter_dimension=0, tiled=True)[0]
    sum_up = lax.psum_scatter(part_up, "fsdp", scatter_dimension=0, tiled=True)[0]
    summed = jnp.concatenate([sum_down, sum_up], axis=1)

    owner_range = jnp.arange(dp_count, dtype=jnp.int32)
    to_owner = my_owner[None, :] == owner_range[:, None]
    pick_index = jnp.sum(jnp.where(to_owner, slot_range[None, :], 0), axis=1)
    owner_has = jnp.any(to_owner, axis=1)
    send_grad = jnp.take(summed.reshape(list_len, rank, down_cols + up_cols), pick_index, axis=0)
    send_grad = jnp.where(owner_has[:, None, None], send_grad, 0.0)
    back_grad = lax.all_to_all(send_grad, "dp", split_axis=0, concat_axis=0, tiled=True)
    land = jnp.where(owned_any, locally_owned_slots, 0)
    arrived = jnp.where(owned_any[:, None, None], back_grad, 0.0)
    grad_down = jnp.zeros((each_owner_rows, rank, down_cols), f32).at[land].add(
        arrived[:, :, :down_cols]
    )
    grad_up = jnp.zeros((each_owner_rows, rank, up_cols), f32).at[land].add(
        arrived[:, :, down_cols:]
    )
    return (value, grad_down, grad_up)


def solution(mesh):
    return jax.shard_map(
        body,
        mesh=mesh,
        in_specs=(
            P(("dp", "fsdp"), None),
            P("fsdp", None),
            P("dp", None, "fsdp"),
            P("dp", None, "fsdp"),
            P(("dp", "fsdp"), None),
            P("dp", None),
            P(),
            P(),
        ),
        out_specs=(P(("dp", "fsdp"), None), P("dp", None, "fsdp"), P("dp", None, "fsdp")),
        check_vma=False,
    )
```

```python
import jax
import jax.numpy as jnp
from jax import lax
from jax.sharding import PartitionSpec as P

WIN = 128


ADAPTER_SCALE = 2.0


def body(
    tokens,
    frozen_value_matrix,
    adapter_down_maps,
    adapter_up_maps,
    value_output_gradient,
    window_composer_position,
    needed_composers,
    composer_storage_index,
):
    f32, bf16 = jnp.float32, jnp.bfloat16
    dp_count = lax.axis_size("dp")
    fsdp_count = lax.axis_size("fsdp")
    group_index = lax.axis_index("dp")
    member_index = lax.axis_index("fsdp")
    tok_rows, width = tokens.shape
    value_cols = frozen_value_matrix.shape[1]
    rank = adapter_down_maps.shape[1]
    each_owner_rows = adapter_down_maps.shape[0]
    down_cols = adapter_down_maps.shape[2]
    up_cols = adapter_up_maps.shape[2]
    list_len = needed_composers.shape[1]
    windows = tok_rows // WIN

    part_cols = value_cols // dp_count
    w_part = lax.dynamic_slice_in_dim(
        frozen_value_matrix, group_index * part_cols, part_cols, axis=1
    )

    list_slot = jnp.take(composer_storage_index, needed_composers, axis=0)
    list_owner = list_slot // each_owner_rows
    list_local = list_slot % each_owner_rows
    owned_here = list_owner == group_index
    locally_owned_slots = jnp.sum(jnp.where(owned_here, list_local, 0), axis=1)
    owned_any = jnp.any(owned_here, axis=1)
    send = jnp.concatenate(
        [
            jnp.take(adapter_down_maps, locally_owned_slots, axis=0),
            jnp.take(adapter_up_maps, locally_owned_slots, axis=0),
        ],
        axis=2,
    )
    send = jnp.where(owned_any[:, None, None], send, jnp.zeros((), send.dtype))
    got = lax.all_to_all(send, "dp", split_axis=0, concat_axis=0, tiled=True)
    my_owner = lax.dynamic_index_in_dim(list_owner, group_index, 0, keepdims=False)
    slab = jnp.take(got, my_owner, axis=0)
    lane = part_cols
    down_rows = list_len * rank * down_cols // lane
    buf = jnp.concatenate(
        [
            w_part,
            slab[..., :down_cols].reshape(down_rows, lane),
            slab[..., down_cols:].reshape(-1, lane),
        ],
        axis=0,
    )
    gathered = lax.all_gather(buf, "fsdp", axis=0, tiled=False)
    w_rows = w_part.shape[0]
    shares_down = gathered[:, w_rows : w_rows + down_rows].reshape(
        fsdp_count, list_len, rank, down_cols
    )
    shares_up = gathered[:, w_rows + down_rows :].reshape(fsdp_count, list_len, rank, up_cols)
    full_down = shares_down.transpose(1, 2, 0, 3).reshape(list_len, rank, width)
    full_up = shares_up.transpose(1, 2, 0, 3).reshape(list_len, rank, value_cols)

    w_part_full = gathered[:, : w_part.shape[0]].reshape(width, part_cols)
    up_x = [(i, (i + 2) % dp_count) for i in range(dp_count)]
    down_x = [(i, (i - 2) % dp_count) for i in range(dp_count)]
    from_left = lax.ppermute(w_part_full, "dp", up_x)
    from_right = lax.ppermute(w_part_full, "dp", down_x)
    half_part = part_cols // 2
    far_a = lax.ppermute(from_left[:, :half_part], "dp", up_x)
    far_b = lax.ppermute(from_right[:, half_part:], "dp", down_x)
    far = jnp.concatenate([far_a, far_b], axis=1)
    same_parity = [w_part_full, from_left, far, from_right]
    w_own = jnp.concatenate(same_parity, axis=1)
    w_partner = lax.ppermute(w_own, "dp", [(i, i ^ 1) for i in range(dp_count)])
    out_own = jnp.dot(tokens, w_own, preferred_element_type=f32)
    out_partner = jnp.dot(tokens, w_partner, preferred_element_type=f32)
    held = jnp.concatenate([out_own, out_partner], axis=1).reshape(tok_rows, dp_count, part_cols)
    part_ids = jnp.arange(dp_count, dtype=jnp.int32)
    partner_index = group_index ^ 1
    same = (part_ids % 2) == (group_index % 2)
    where_held = jnp.where(
        same,
        ((group_index - part_ids) % dp_count) // 2,
        dp_count // 2 + ((partner_index - part_ids) % dp_count) // 2,
    )
    frozen_rows = jnp.take(held, where_held, axis=1).reshape(tok_rows, value_cols)

    group_picks = window_composer_position[0]
    my_picks = lax.dynamic_slice_in_dim(group_picks, member_index * windows, windows, 0)
    slot_range = jnp.arange(list_len, dtype=jnp.int32)
    token_hot = jnp.broadcast_to(
        my_picks[:, None, None] == slot_range[None, None, :], (windows, WIN, list_len)
    ).reshape(tok_rows, list_len)
    hot_f = token_hot.astype(f32)

    down_flat = full_down.reshape(list_len * rank, width)
    up_flat = full_up.reshape(list_len * rank, value_cols)
    low_all = lax.dot_general(
        tokens, down_flat, (((1,), (1,)), ((), ())), preferred_element_type=f32
    ).reshape(tok_rows, list_len, rank)
    low = jnp.sum(low_all * hot_f[:, :, None], axis=1).astype(bf16)
    hot_h = token_hot.astype(bf16)
    masked_low = (hot_h[:, :, None] * low[:, None, :]).reshape(tok_rows, list_len * rank)
    adapter_change = jnp.dot(masked_low, up_flat, preferred_element_type=f32)
    value = (frozen_rows + ADAPTER_SCALE * adapter_change).astype(bf16)

    back_all = lax.dot_general(
        value_output_gradient, up_flat, (((1,), (1,)), ((), ())), preferred_element_type=f32
    ).reshape(tok_rows, list_len, rank)
    back = (ADAPTER_SCALE * jnp.sum(back_all * hot_f[:, :, None], axis=1)).astype(bf16)
    masked_back = (hot_h[:, :, None] * back[:, None, :]).reshape(tok_rows, list_len * rank)
    scaled_masked_low = masked_low * jnp.asarray(ADAPTER_SCALE, bf16)

    contract = (((0,), (0,)), ((), ()))
    part_down = lax.dot_general(masked_back, tokens, contract, preferred_element_type=f32)
    part_up = lax.dot_general(
        scaled_masked_low, value_output_gradient, contract, preferred_element_type=f32
    )
    rows = list_len * rank
    part_down = part_down.reshape(rows, fsdp_count, down_cols).transpose(1, 0, 2)
    part_up = part_up.reshape(rows, fsdp_count, up_cols).transpose(1, 0, 2)
    sum_down = lax.psum_scatter(part_down, "fsdp", scatter_dimension=0, tiled=True)[0]
    sum_up = jnp.sum(lax.all_to_all(part_up, "fsdp", 0, 0, tiled=True), axis=0)
    summed = jnp.concatenate([sum_down, sum_up], axis=1)

    owner_range = jnp.arange(dp_count, dtype=jnp.int32)
    to_owner = my_owner[None, :] == owner_range[:, None]
    pick_index = jnp.sum(jnp.where(to_owner, slot_range[None, :], 0), axis=1)
    owner_has = jnp.any(to_owner, axis=1)
    send_grad = jnp.take(summed.reshape(list_len, rank, down_cols + up_cols), pick_index, axis=0)
    send_grad = jnp.where(owner_has[:, None, None], send_grad, 0.0)
    back_grad = lax.all_to_all(send_grad, "dp", split_axis=0, concat_axis=0, tiled=True)
    land = jnp.where(owned_any, locally_owned_slots, 0)
    arrived = jnp.where(owned_any[:, None, None], back_grad, 0.0)
    grad_down = jnp.zeros((each_owner_rows, rank, down_cols), f32).at[land].add(
        arrived[:, :, :down_cols]
    )
    grad_up = jnp.zeros((each_owner_rows, rank, up_cols), f32).at[land].add(
        arrived[:, :, down_cols:]
    )
    return (value, grad_down, grad_up)


def solution(mesh):
    return jax.shard_map(
        body,
        mesh=mesh,
        in_specs=(
            P(("dp", "fsdp"), None),
            P("fsdp", None),
            P("dp", None, "fsdp"),
            P("dp", None, "fsdp"),
            P(("dp", "fsdp"), None),
            P("dp", None),
            P(),
            P(),
        ),
        out_specs=(P(("dp", "fsdp"), None), P("dp", None, "fsdp"), P("dp", None, "fsdp")),
        check_vma=False,
    )
```

```python
import jax
import jax.numpy as jnp
from jax import lax
from jax.sharding import PartitionSpec as P

WIN = 128


ADAPTER_SCALE = 2.0


def body(
    tokens,
    frozen_value_matrix,
    adapter_down_maps,
    adapter_up_maps,
    value_output_gradient,
    window_composer_position,
    needed_composers,
    composer_storage_index,
):
    f32, bf16 = jnp.float32, jnp.bfloat16
    dp_count = lax.axis_size("dp")
    fsdp_count = lax.axis_size("fsdp")
    group_index = lax.axis_index("dp")
    member_index = lax.axis_index("fsdp")
    tok_rows, width = tokens.shape
    value_cols = frozen_value_matrix.shape[1]
    rank = adapter_down_maps.shape[1]
    each_owner_rows = adapter_down_maps.shape[0]
    down_cols = adapter_down_maps.shape[2]
    up_cols = adapter_up_maps.shape[2]
    list_len = needed_composers.shape[1]
    windows = tok_rows // WIN

    part_cols = value_cols // dp_count
    w_part = lax.dynamic_slice_in_dim(
        frozen_value_matrix, group_index * part_cols, part_cols, axis=1
    )

    list_slot = jnp.take(composer_storage_index, needed_composers, axis=0)
    list_owner = list_slot // each_owner_rows
    list_local = list_slot % each_owner_rows
    owned_here = list_owner == group_index
    locally_owned_slots = jnp.sum(jnp.where(owned_here, list_local, 0), axis=1)
    owned_any = jnp.any(owned_here, axis=1)
    down_sel = jnp.take(adapter_down_maps, locally_owned_slots, axis=0)
    up_sel = jnp.take(adapter_up_maps, locally_owned_slots, axis=0)
    pad_cols = (-(down_cols + up_cols)) % 128
    send = jnp.concatenate(
        [down_sel, up_sel, jnp.zeros(up_sel.shape[:2] + (pad_cols,), up_sel.dtype)], axis=2
    )
    send = jnp.where(owned_any[:, None, None], send, jnp.zeros((), send.dtype))
    got = lax.all_to_all(send, "dp", split_axis=0, concat_axis=0, tiled=True)
    my_owner = lax.dynamic_index_in_dim(list_owner, group_index, 0, keepdims=False)
    slab = jnp.take(got, my_owner, axis=0)
    slab_cols = slab.shape[2]
    w_as_slab = w_part.reshape(list_len, rank, -1)
    buf = jnp.concatenate([slab, w_as_slab], axis=2)
    buf_cols = buf.shape[2]
    gathered = lax.all_gather(buf, "fsdp", axis=2, tiled=True).reshape(
        list_len, rank, fsdp_count, buf_cols
    )
    full_down = gathered[..., :down_cols].reshape(list_len, rank, width)
    full_up = gathered[..., down_cols : down_cols + up_cols].reshape(list_len, rank, value_cols)
    w_part_full = (
        gathered[..., slab_cols:].transpose(2, 0, 1, 3).reshape(width, part_cols)
    )

    up_x = [(i, (i + 2) % dp_count) for i in range(dp_count)]
    down_x = [(i, (i - 2) % dp_count) for i in range(dp_count)]
    from_left = lax.ppermute(w_part_full, "dp", up_x)
    from_right = lax.ppermute(w_part_full, "dp", down_x)
    half_part = part_cols // 2
    far_a = lax.ppermute(from_left[:, :half_part], "dp", up_x)
    far_b = lax.ppermute(from_right[:, half_part:], "dp", down_x)
    far = jnp.concatenate([far_a, far_b], axis=1)
    same_parity = [w_part_full, from_left, far, from_right]
    w_own = jnp.concatenate(same_parity, axis=1)
    w_partner = lax.ppermute(w_own, "dp", [(i, i ^ 1) for i in range(dp_count)])
    out_own = jnp.dot(tokens, w_own, preferred_element_type=f32)
    out_partner = jnp.dot(tokens, w_partner, preferred_element_type=f32)
    held = jnp.concatenate([out_own, out_partner], axis=1).reshape(tok_rows, dp_count, part_cols)
    part_ids = jnp.arange(dp_count, dtype=jnp.int32)
    partner_index = group_index ^ 1
    same = (part_ids % 2) == (group_index % 2)
    where_held = jnp.where(
        same,
        ((group_index - part_ids) % dp_count) // 2,
        dp_count // 2 + ((partner_index - part_ids) % dp_count) // 2,
    )
    frozen_rows = jnp.take(held, where_held, axis=1).reshape(tok_rows, value_cols)

    group_picks = window_composer_position[0]
    my_picks = lax.dynamic_slice_in_dim(group_picks, member_index * windows, windows, 0)
    slot_range = jnp.arange(list_len, dtype=jnp.int32)
    token_hot = jnp.broadcast_to(
        my_picks[:, None, None] == slot_range[None, None, :], (windows, WIN, list_len)
    ).reshape(tok_rows, list_len)
    hot_f = token_hot.astype(f32)

    down_flat = full_down.reshape(list_len * rank, width)
    up_flat = full_up.reshape(list_len * rank, value_cols)
    low_all = lax.dot_general(
        tokens, down_flat, (((1,), (1,)), ((), ())), preferred_element_type=f32
    ).reshape(tok_rows, list_len, rank)
    low = jnp.sum(low_all * hot_f[:, :, None], axis=1).astype(bf16)
    hot_h = token_hot.astype(bf16)
    masked_low = (hot_h[:, :, None] * low[:, None, :]).reshape(tok_rows, list_len * rank)
    adapter_change = jnp.dot(masked_low, up_flat, preferred_element_type=f32)
    value = (frozen_rows + ADAPTER_SCALE * adapter_change).astype(bf16)

    back_all = lax.dot_general(
        value_output_gradient, up_flat, (((1,), (1,)), ((), ())), preferred_element_type=f32
    ).reshape(tok_rows, list_len, rank)
    back = (ADAPTER_SCALE * jnp.sum(back_all * hot_f[:, :, None], axis=1)).astype(bf16)
    masked_back = (hot_h[:, :, None] * back[:, None, :]).reshape(tok_rows, list_len * rank)
    scaled_masked_low = masked_low * jnp.asarray(ADAPTER_SCALE, bf16)

    contract = (((0,), (0,)), ((), ()))
    part_down = lax.dot_general(masked_back, tokens, contract, preferred_element_type=f32)
    part_up = lax.dot_general(
        scaled_masked_low, value_output_gradient, contract, preferred_element_type=f32
    )
    rows = list_len * rank
    part_up = part_up.reshape(rows, fsdp_count, up_cols).transpose(1, 0, 2)
    sum_down = lax.psum_scatter(part_down, "fsdp", scatter_dimension=1, tiled=True)
    sum_up = jnp.sum(lax.all_to_all(part_up, "fsdp", 0, 0, tiled=True), axis=0)
    summed = jnp.concatenate([sum_down, sum_up], axis=1)

    owner_range = jnp.arange(dp_count, dtype=jnp.int32)
    to_owner = my_owner[None, :] == owner_range[:, None]
    pick_index = jnp.sum(jnp.where(to_owner, slot_range[None, :], 0), axis=1)
    owner_has = jnp.any(to_owner, axis=1)
    send_grad = jnp.take(summed.reshape(list_len, rank, down_cols + up_cols), pick_index, axis=0)
    send_grad = jnp.where(owner_has[:, None, None], send_grad, 0.0)
    back_grad = lax.all_to_all(send_grad, "dp", split_axis=0, concat_axis=0, tiled=True)
    land = jnp.where(owned_any, locally_owned_slots, 0)
    arrived = jnp.where(owned_any[:, None, None], back_grad, 0.0)
    grad_down = jnp.zeros((each_owner_rows, rank, down_cols), f32).at[land].add(
        arrived[:, :, :down_cols]
    )
    grad_up = jnp.zeros((each_owner_rows, rank, up_cols), f32).at[land].add(
        arrived[:, :, down_cols:]
    )
    return (value, grad_down, grad_up)


def solution(mesh):
    return jax.shard_map(
        body,
        mesh=mesh,
        in_specs=(
            P(("dp", "fsdp"), None),
            P("fsdp", None),
            P("dp", None, "fsdp"),
            P("dp", None, "fsdp"),
            P(("dp", "fsdp"), None),
            P("dp", None),
            P(),
            P(),
        ),
        out_specs=(P(("dp", "fsdp"), None), P("dp", None, "fsdp"), P("dp", None, "fsdp")),
        check_vma=False,
    )
```

```python
import jax
import jax.numpy as jnp
from jax import lax
from jax.sharding import PartitionSpec as P

WIN = 128


ADAPTER_SCALE = 2.0


def body(
    tokens,
    frozen_value_matrix,
    adapter_down_maps,
    adapter_up_maps,
    value_output_gradient,
    window_composer_position,
    needed_composers,
    composer_storage_index,
):
    f32, bf16 = jnp.float32, jnp.bfloat16
    dp_count = lax.axis_size("dp")
    fsdp_count = lax.axis_size("fsdp")
    group_index = lax.axis_index("dp")
    member_index = lax.axis_index("fsdp")
    tok_rows, width = tokens.shape
    value_cols = frozen_value_matrix.shape[1]
    rank = adapter_down_maps.shape[1]
    each_owner_rows = adapter_down_maps.shape[0]
    down_cols = adapter_down_maps.shape[2]
    up_cols = adapter_up_maps.shape[2]
    list_len = needed_composers.shape[1]
    windows = tok_rows // WIN

    part_cols = value_cols // dp_count
    w_part = lax.dynamic_slice_in_dim(
        frozen_value_matrix, group_index * part_cols, part_cols, axis=1
    )
    w_part_full = lax.all_gather(w_part, "fsdp", axis=0, tiled=True)
    up_x = [(i, (i + 2) % dp_count) for i in range(dp_count)]
    down_x = [(i, (i - 2) % dp_count) for i in range(dp_count)]
    from_left = lax.ppermute(w_part_full, "dp", up_x)
    from_right = lax.ppermute(w_part_full, "dp", down_x)
    half_part = part_cols // 2
    far_a = lax.ppermute(from_left[:, :half_part], "dp", up_x)
    far_b = lax.ppermute(from_right[:, half_part:], "dp", down_x)
    far = jnp.concatenate([far_a, far_b], axis=1)
    same_parity = [w_part_full, from_left, far, from_right]
    w_own = jnp.concatenate(same_parity, axis=1)
    w_partner = lax.ppermute(w_own, "dp", [(i, i ^ 1) for i in range(dp_count)])
    out_own = jnp.dot(tokens, w_own, preferred_element_type=f32)
    out_partner = jnp.dot(tokens, w_partner, preferred_element_type=f32)
    held = jnp.concatenate([out_own, out_partner], axis=1).reshape(tok_rows, dp_count, part_cols)
    part_ids = jnp.arange(dp_count, dtype=jnp.int32)
    partner_index = group_index ^ 1
    same = (part_ids % 2) == (group_index % 2)
    where_held = jnp.where(
        same,
        ((group_index - part_ids) % dp_count) // 2,
        dp_count // 2 + ((partner_index - part_ids) % dp_count) // 2,
    )
    frozen_rows = jnp.take(held, where_held, axis=1).reshape(tok_rows, value_cols)

    list_slot = jnp.take(composer_storage_index, needed_composers, axis=0)
    list_owner = list_slot // each_owner_rows
    list_local = list_slot % each_owner_rows
    owned_here = list_owner == group_index
    locally_owned_slots = jnp.sum(jnp.where(owned_here, list_local, 0), axis=1)
    owned_any = jnp.any(owned_here, axis=1)
    send = jnp.concatenate(
        [
            jnp.take(adapter_down_maps, locally_owned_slots, axis=0),
            jnp.take(adapter_up_maps, locally_owned_slots, axis=0),
        ],
        axis=2,
    )
    send = jnp.where(owned_any[:, None, None], send, jnp.zeros((), send.dtype))
    got = lax.all_to_all(send, "dp", split_axis=0, concat_axis=0, tiled=True)
    my_owner = lax.dynamic_index_in_dim(list_owner, group_index, 0, keepdims=False)
    slab = jnp.take(got, my_owner, axis=0)
    shares = lax.all_gather(slab, "fsdp", axis=0, tiled=False)
    full_down = shares[..., :down_cols].transpose(1, 2, 0, 3).reshape(list_len, rank, width)
    full_up = shares[..., down_cols:].transpose(1, 2, 0, 3).reshape(list_len, rank, value_cols)

    group_picks = window_composer_position[0]
    my_picks = lax.dynamic_slice_in_dim(group_picks, member_index * windows, windows, 0)
    slot_range = jnp.arange(list_len, dtype=jnp.int32)
    token_hot = jnp.broadcast_to(
        my_picks[:, None, None] == slot_range[None, None, :], (windows, WIN, list_len)
    ).reshape(tok_rows, list_len)
    hot_f = token_hot.astype(f32)

    down_flat = full_down.reshape(list_len * rank, width)
    up_flat = full_up.reshape(list_len * rank, value_cols)
    low_all = lax.dot_general(
        tokens, down_flat, (((1,), (1,)), ((), ())), preferred_element_type=f32
    ).reshape(tok_rows, list_len, rank)
    low = jnp.sum(low_all * hot_f[:, :, None], axis=1).astype(bf16)
    hot_h = token_hot.astype(bf16)
    masked_low = (hot_h[:, :, None] * low[:, None, :]).reshape(tok_rows, list_len * rank)
    adapter_change = jnp.dot(masked_low, up_flat, preferred_element_type=f32)
    value = (frozen_rows + ADAPTER_SCALE * adapter_change).astype(bf16)

    back_all = lax.dot_general(
        value_output_gradient, up_flat, (((1,), (1,)), ((), ())), preferred_element_type=f32
    ).reshape(tok_rows, list_len, rank)
    back = (ADAPTER_SCALE * jnp.sum(back_all * hot_f[:, :, None], axis=1)).astype(bf16)
    masked_back = (hot_h[:, :, None] * back[:, None, :]).reshape(tok_rows, list_len * rank)
    scaled_masked_low = masked_low * jnp.asarray(ADAPTER_SCALE, bf16)

    contract = (((0,), (0,)), ((), ()))
    part_down = lax.dot_general(masked_back, tokens, contract, preferred_element_type=f32)
    part_up = lax.dot_general(
        scaled_masked_low, value_output_gradient, contract, preferred_element_type=f32
    )
    rows = list_len * rank
    part_down = part_down.reshape(rows, fsdp_count, down_cols).transpose(1, 0, 2)
    part_up = part_up.reshape(rows, fsdp_count, up_cols).transpose(1, 0, 2)
    summed = lax.psum_scatter(
        jnp.concatenate([part_down, part_up], axis=2), "fsdp", scatter_dimension=0, tiled=True
    )[0]

    owner_range = jnp.arange(dp_count, dtype=jnp.int32)
    to_owner = my_owner[None, :] == owner_range[:, None]
    pick_index = jnp.sum(jnp.where(to_owner, slot_range[None, :], 0), axis=1)
    owner_has = jnp.any(to_owner, axis=1)
    send_grad = jnp.take(summed.reshape(list_len, rank, down_cols + up_cols), pick_index, axis=0)
    send_grad = jnp.where(owner_has[:, None, None], send_grad, 0.0)
    back_grad = lax.all_to_all(send_grad, "dp", split_axis=0, concat_axis=0, tiled=True)
    land = jnp.where(owned_any, locally_owned_slots, 0)
    arrived = jnp.where(owned_any[:, None, None], back_grad, 0.0)
    grad_down = jnp.zeros((each_owner_rows, rank, down_cols), f32).at[land].add(
        arrived[:, :, :down_cols]
    )
    grad_up = jnp.zeros((each_owner_rows, rank, up_cols), f32).at[land].add(
        arrived[:, :, down_cols:]
    )
    return (value, grad_down, grad_up)


def solution(mesh):
    return jax.shard_map(
        body,
        mesh=mesh,
        in_specs=(
            P(("dp", "fsdp"), None),
            P("fsdp", None),
            P("dp", None, "fsdp"),
            P("dp", None, "fsdp"),
            P(("dp", "fsdp"), None),
            P("dp", None),
            P(),
            P(),
        ),
        out_specs=(P(("dp", "fsdp"), None), P("dp", None, "fsdp"), P("dp", None, "fsdp")),
        check_vma=False,
    )
```

```python
import jax
import jax.numpy as jnp
from jax import lax
from jax.sharding import PartitionSpec as P

WIN = 128


ADAPTER_SCALE = 2.0


def body(
    tokens,
    frozen_value_matrix,
    adapter_down_maps,
    adapter_up_maps,
    value_output_gradient,
    window_composer_position,
    needed_composers,
    composer_storage_index,
):
    f32, bf16 = jnp.float32, jnp.bfloat16
    dp_count = lax.axis_size("dp")
    fsdp_count = lax.axis_size("fsdp")
    group_index = lax.axis_index("dp")
    member_index = lax.axis_index("fsdp")
    tok_rows, width = tokens.shape
    value_cols = frozen_value_matrix.shape[1]
    rank = adapter_down_maps.shape[1]
    each_owner_rows = adapter_down_maps.shape[0]
    down_cols = adapter_down_maps.shape[2]
    up_cols = adapter_up_maps.shape[2]
    list_len = needed_composers.shape[1]
    windows = tok_rows // WIN

    part_cols = value_cols // dp_count
    w_part = lax.dynamic_slice_in_dim(
        frozen_value_matrix, group_index * part_cols, part_cols, axis=1
    )
    w_part_full = lax.all_gather(w_part, "fsdp", axis=0, tiled=True)
    up_x = [(i, (i + 2) % dp_count) for i in range(dp_count)]
    down_x = [(i, (i - 2) % dp_count) for i in range(dp_count)]
    from_left = lax.ppermute(w_part_full, "dp", up_x)
    from_right = lax.ppermute(w_part_full, "dp", down_x)
    half_part = part_cols // 2
    far_a = lax.ppermute(from_left[:, :half_part], "dp", up_x)
    far_b = lax.ppermute(from_right[:, half_part:], "dp", down_x)
    far = jnp.concatenate([far_a, far_b], axis=1)
    same_parity = [w_part_full, from_left, far, from_right]
    pair = [(i, i ^ 1) for i in range(dp_count)]
    w_own = jnp.concatenate(same_parity, axis=1)
    w_partner = jnp.concatenate([lax.ppermute(p, "dp", pair) for p in same_parity], axis=1)
    out_own = jnp.dot(tokens, w_own, preferred_element_type=f32)
    out_partner = jnp.dot(tokens, w_partner, preferred_element_type=f32)
    held = jnp.concatenate([out_own, out_partner], axis=1).reshape(tok_rows, dp_count, part_cols)
    part_ids = jnp.arange(dp_count, dtype=jnp.int32)
    partner_index = group_index ^ 1
    same = (part_ids % 2) == (group_index % 2)
    where_held = jnp.where(
        same,
        ((group_index - part_ids) % dp_count) // 2,
        dp_count // 2 + ((partner_index - part_ids) % dp_count) // 2,
    )
    frozen_rows = jnp.take(held, where_held, axis=1).reshape(tok_rows, value_cols)

    list_slot = jnp.take(composer_storage_index, needed_composers, axis=0)
    list_owner = list_slot // each_owner_rows
    list_local = list_slot % each_owner_rows
    owned_here = list_owner == group_index
    locally_owned_slots = jnp.sum(jnp.where(owned_here, list_local, 0), axis=1)
    owned_any = jnp.any(owned_here, axis=1)
    send = jnp.concatenate(
        [
            jnp.take(adapter_down_maps, locally_owned_slots, axis=0),
            jnp.take(adapter_up_maps, locally_owned_slots, axis=0),
        ],
        axis=2,
    )
    send = jnp.where(owned_any[:, None, None], send, jnp.zeros((), send.dtype))
    got = lax.all_to_all(send, "dp", split_axis=0, concat_axis=0, tiled=True)
    my_owner = lax.dynamic_index_in_dim(list_owner, group_index, 0, keepdims=False)
    slab = jnp.take(got, my_owner, axis=0)
    shares = lax.all_gather(slab, "fsdp", axis=0, tiled=False)
    full_down = shares[..., :down_cols].transpose(1, 2, 0, 3).reshape(list_len, rank, width)
    full_up = shares[..., down_cols:].transpose(1, 2, 0, 3).reshape(list_len, rank, value_cols)

    group_picks = window_composer_position[0]
    my_picks = lax.dynamic_slice_in_dim(group_picks, member_index * windows, windows, 0)
    slot_range = jnp.arange(list_len, dtype=jnp.int32)
    token_hot = jnp.broadcast_to(
        my_picks[:, None, None] == slot_range[None, None, :], (windows, WIN, list_len)
    ).reshape(tok_rows, list_len)
    hot_f = token_hot.astype(f32)

    down_flat = full_down.reshape(list_len * rank, width)
    up_flat = full_up.reshape(list_len * rank, value_cols)
    low_all = lax.dot_general(
        tokens, down_flat, (((1,), (1,)), ((), ())), preferred_element_type=f32
    ).reshape(tok_rows, list_len, rank)
    low = jnp.sum(low_all * hot_f[:, :, None], axis=1).astype(bf16)
    hot_h = token_hot.astype(bf16)
    masked_low = (hot_h[:, :, None] * low[:, None, :]).reshape(tok_rows, list_len * rank)
    adapter_change = jnp.dot(masked_low, up_flat, preferred_element_type=f32)
    value = (frozen_rows + ADAPTER_SCALE * adapter_change).astype(bf16)

    back_all = lax.dot_general(
        value_output_gradient, up_flat, (((1,), (1,)), ((), ())), preferred_element_type=f32
    ).reshape(tok_rows, list_len, rank)
    back = (ADAPTER_SCALE * jnp.sum(back_all * hot_f[:, :, None], axis=1)).astype(bf16)
    masked_back = (hot_h[:, :, None] * back[:, None, :]).reshape(tok_rows, list_len * rank)
    scaled_masked_low = masked_low * jnp.asarray(ADAPTER_SCALE, bf16)

    contract = (((0,), (0,)), ((), ()))
    part_down = lax.dot_general(masked_back, tokens, contract, preferred_element_type=f32)
    part_up = lax.dot_general(
        scaled_masked_low, value_output_gradient, contract, preferred_element_type=f32
    )
    rows = list_len * rank
    part_down = part_down.reshape(rows, fsdp_count, down_cols).transpose(1, 0, 2)
    part_up = part_up.reshape(rows, fsdp_count, up_cols).transpose(1, 0, 2)
    summed = lax.psum_scatter(
        jnp.concatenate([part_down, part_up], axis=2), "fsdp", scatter_dimension=0, tiled=True
    )[0]

    owner_range = jnp.arange(dp_count, dtype=jnp.int32)
    to_owner = my_owner[None, :] == owner_range[:, None]
    pick_index = jnp.sum(jnp.where(to_owner, slot_range[None, :], 0), axis=1)
    owner_has = jnp.any(to_owner, axis=1)
    send_grad = jnp.take(summed.reshape(list_len, rank, down_cols + up_cols), pick_index, axis=0)
    send_grad = jnp.where(owner_has[:, None, None], send_grad, 0.0)
    back_grad = lax.all_to_all(send_grad, "dp", split_axis=0, concat_axis=0, tiled=True)
    land = jnp.where(owned_any, locally_owned_slots, 0)
    arrived = jnp.where(owned_any[:, None, None], back_grad, 0.0)
    grad_down = jnp.zeros((each_owner_rows, rank, down_cols), f32).at[land].add(
        arrived[:, :, :down_cols]
    )
    grad_up = jnp.zeros((each_owner_rows, rank, up_cols), f32).at[land].add(
        arrived[:, :, down_cols:]
    )
    return (value, grad_down, grad_up)


def solution(mesh):
    return jax.shard_map(
        body,
        mesh=mesh,
        in_specs=(
            P(("dp", "fsdp"), None),
            P("fsdp", None),
            P("dp", None, "fsdp"),
            P("dp", None, "fsdp"),
            P(("dp", "fsdp"), None),
            P("dp", None),
            P(),
            P(),
        ),
        out_specs=(P(("dp", "fsdp"), None), P("dp", None, "fsdp"), P("dp", None, "fsdp")),
        check_vma=False,
    )
```

```python
import jax
import jax.numpy as jnp
from jax import lax
from jax.sharding import PartitionSpec as P

WIN = 128


ADAPTER_SCALE = 2.0


def body(
    tokens,
    frozen_value_matrix,
    adapter_down_maps,
    adapter_up_maps,
    value_output_gradient,
    window_composer_position,
    needed_composers,
    composer_storage_index,
):
    f32, bf16 = jnp.float32, jnp.bfloat16
    dp_count = lax.axis_size("dp")
    fsdp_count = lax.axis_size("fsdp")
    group_index = lax.axis_index("dp")
    member_index = lax.axis_index("fsdp")
    tok_rows, width = tokens.shape
    value_cols = frozen_value_matrix.shape[1]
    rank = adapter_down_maps.shape[1]
    each_owner_rows = adapter_down_maps.shape[0]
    down_cols = adapter_down_maps.shape[2]
    up_cols = adapter_up_maps.shape[2]
    list_len = needed_composers.shape[1]
    windows = tok_rows // WIN

    part_cols = value_cols // dp_count
    w_part = lax.dynamic_slice_in_dim(
        frozen_value_matrix, group_index * part_cols, part_cols, axis=1
    )
    w_part_full = lax.all_gather(w_part, "fsdp", axis=0, tiled=True)
    up_x = [(i, (i + 2) % dp_count) for i in range(dp_count)]
    down_x = [(i, (i - 2) % dp_count) for i in range(dp_count)]
    from_left = lax.ppermute(w_part_full, "dp", up_x)
    from_right = lax.ppermute(w_part_full, "dp", down_x)
    half_part = part_cols // 2
    far_a = lax.ppermute(from_left[:, :half_part], "dp", up_x)
    far_b = lax.ppermute(from_right[:, half_part:], "dp", down_x)
    far = jnp.concatenate([far_a, far_b], axis=1)
    same_parity = [w_part_full, from_left, far, from_right]
    w_own = jnp.concatenate(same_parity, axis=1)
    w_partner = lax.ppermute(w_own, "dp", [(i, i ^ 1) for i in range(dp_count)])
    out_own = jnp.dot(tokens, w_own, preferred_element_type=f32)
    out_partner = jnp.dot(tokens, w_partner, preferred_element_type=f32)
    held = jnp.concatenate([out_own, out_partner], axis=1).reshape(tok_rows, dp_count, part_cols)
    part_ids = jnp.arange(dp_count, dtype=jnp.int32)
    partner_index = group_index ^ 1
    same = (part_ids % 2) == (group_index % 2)
    where_held = jnp.where(
        same,
        ((group_index - part_ids) % dp_count) // 2,
        dp_count // 2 + ((partner_index - part_ids) % dp_count) // 2,
    )
    frozen_rows = jnp.take(held, where_held, axis=1).reshape(tok_rows, value_cols)

    list_slot = jnp.take(composer_storage_index, needed_composers, axis=0)
    list_owner = list_slot // each_owner_rows
    list_local = list_slot % each_owner_rows
    owned_here = list_owner == group_index
    locally_owned_slots = jnp.sum(jnp.where(owned_here, list_local, 0), axis=1)
    owned_any = jnp.any(owned_here, axis=1)
    send = jnp.concatenate(
        [
            jnp.take(adapter_down_maps, locally_owned_slots, axis=0),
            jnp.take(adapter_up_maps, locally_owned_slots, axis=0),
        ],
        axis=2,
    )
    send = jnp.where(owned_any[:, None, None], send, jnp.zeros((), send.dtype))
    got = lax.all_to_all(send, "dp", split_axis=0, concat_axis=0, tiled=True)
    my_owner = lax.dynamic_index_in_dim(list_owner, group_index, 0, keepdims=False)
    slab = jnp.take(got, my_owner, axis=0)
    shares = lax.all_gather(slab, "fsdp", axis=0, tiled=False)
    full_down = shares[..., :down_cols].transpose(1, 2, 0, 3).reshape(list_len, rank, width)
    full_up = shares[..., down_cols:].transpose(1, 2, 0, 3).reshape(list_len, rank, value_cols)

    group_picks = window_composer_position[0]
    my_picks = lax.dynamic_slice_in_dim(group_picks, member_index * windows, windows, 0)
    slot_range = jnp.arange(list_len, dtype=jnp.int32)
    token_hot = jnp.broadcast_to(
        my_picks[:, None, None] == slot_range[None, None, :], (windows, WIN, list_len)
    ).reshape(tok_rows, list_len)
    hot_f = token_hot.astype(f32)

    down_flat = full_down.reshape(list_len * rank, width)
    up_flat = full_up.reshape(list_len * rank, value_cols)
    low_all = lax.dot_general(
        tokens, down_flat, (((1,), (1,)), ((), ())), preferred_element_type=f32
    ).reshape(tok_rows, list_len, rank)
    low = jnp.sum(low_all * hot_f[:, :, None], axis=1).astype(bf16)
    hot_h = token_hot.astype(bf16)
    masked_low = (hot_h[:, :, None] * low[:, None, :]).reshape(tok_rows, list_len * rank)
    adapter_change = jnp.dot(masked_low, up_flat, preferred_element_type=f32)
    value = (frozen_rows + ADAPTER_SCALE * adapter_change).astype(bf16)

    back_all = lax.dot_general(
        value_output_gradient, up_flat, (((1,), (1,)), ((), ())), preferred_element_type=f32
    ).reshape(tok_rows, list_len, rank)
    back = (ADAPTER_SCALE * jnp.sum(back_all * hot_f[:, :, None], axis=1)).astype(bf16)
    masked_back = (hot_h[:, :, None] * back[:, None, :]).reshape(tok_rows, list_len * rank)
    scaled_masked_low = masked_low * jnp.asarray(ADAPTER_SCALE, bf16)

    contract = (((0,), (0,)), ((), ()))
    part_down = lax.dot_general(masked_back, tokens, contract, preferred_element_type=f32)
    part_up = lax.dot_general(
        scaled_masked_low, value_output_gradient, contract, preferred_element_type=f32
    )
    rows = list_len * rank
    up_rows = rows * up_cols // down_cols
    up_as_rows = (
        part_up.reshape(rows, fsdp_count, up_cols)
        .transpose(1, 0, 2)
        .reshape(fsdp_count, up_rows, down_cols)
        .transpose(1, 0, 2)
        .reshape(up_rows, fsdp_count * down_cols)
    )
    both = jnp.concatenate([part_down, up_as_rows], axis=0)
    summed = lax.psum_scatter(both, "fsdp", scatter_dimension=1, tiled=True)
    per_slot = jnp.concatenate(
        [
            summed[:rows].reshape(list_len, rank, down_cols),
            summed[rows:].reshape(list_len, up_rows // list_len, down_cols),
        ],
        axis=1,
    )

    owner_range = jnp.arange(dp_count, dtype=jnp.int32)
    to_owner = my_owner[None, :] == owner_range[:, None]
    pick_index = jnp.sum(jnp.where(to_owner, slot_range[None, :], 0), axis=1)
    owner_has = jnp.any(to_owner, axis=1)
    send_grad = jnp.take(per_slot, pick_index, axis=0)
    send_grad = jnp.where(owner_has[:, None, None], send_grad, 0.0)
    back_grad = lax.all_to_all(send_grad, "dp", split_axis=0, concat_axis=0, tiled=True)
    land = jnp.where(owned_any, locally_owned_slots, 0)
    arrived = jnp.where(owned_any[:, None, None], back_grad, 0.0)
    grad_down = jnp.zeros((each_owner_rows, rank, down_cols), f32).at[land].add(
        arrived[:, :rank]
    )
    grad_up = jnp.zeros((each_owner_rows, rank, up_cols), f32).at[land].add(
        arrived[:, rank:].reshape(dp_count, rank, up_cols)
    )
    return (value, grad_down, grad_up)


def solution(mesh):
    return jax.shard_map(
        body,
        mesh=mesh,
        in_specs=(
            P(("dp", "fsdp"), None),
            P("fsdp", None),
            P("dp", None, "fsdp"),
            P("dp", None, "fsdp"),
            P(("dp", "fsdp"), None),
            P("dp", None),
            P(),
            P(),
        ),
        out_specs=(P(("dp", "fsdp"), None), P("dp", None, "fsdp"), P("dp", None, "fsdp")),
        check_vma=False,
    )
```

```python
import jax
import jax.numpy as jnp
from jax import lax
from jax.sharding import PartitionSpec as P

WIN = 128


ADAPTER_SCALE = 2.0


def body(
    tokens,
    frozen_value_matrix,
    adapter_down_maps,
    adapter_up_maps,
    value_output_gradient,
    window_composer_position,
    needed_composers,
    composer_storage_index,
):
    f32, bf16 = jnp.float32, jnp.bfloat16
    dp_count = lax.axis_size("dp")
    fsdp_count = lax.axis_size("fsdp")
    group_index = lax.axis_index("dp")
    member_index = lax.axis_index("fsdp")
    tok_rows, width = tokens.shape
    value_cols = frozen_value_matrix.shape[1]
    rank = adapter_down_maps.shape[1]
    each_owner_rows = adapter_down_maps.shape[0]
    down_cols = adapter_down_maps.shape[2]
    up_cols = adapter_up_maps.shape[2]
    list_len = needed_composers.shape[1]
    windows = tok_rows // WIN

    part_cols = value_cols // dp_count
    w_part = lax.dynamic_slice_in_dim(
        frozen_value_matrix, group_index * part_cols, part_cols, axis=1
    )

    list_slot = jnp.take(composer_storage_index, needed_composers, axis=0)
    list_owner = list_slot // each_owner_rows
    list_local = list_slot % each_owner_rows
    owned_here = list_owner == group_index
    locally_owned_slots = jnp.sum(jnp.where(owned_here, list_local, 0), axis=1)
    owned_any = jnp.any(owned_here, axis=1)
    send = jnp.concatenate(
        [
            jnp.take(adapter_down_maps, locally_owned_slots, axis=0),
            jnp.take(adapter_up_maps, locally_owned_slots, axis=0),
        ],
        axis=2,
    )
    send = jnp.where(owned_any[:, None, None], send, jnp.zeros((), send.dtype))
    got = lax.all_to_all(send, "dp", split_axis=0, concat_axis=0, tiled=True)
    my_owner = lax.dynamic_index_in_dim(list_owner, group_index, 0, keepdims=False)
    slab = jnp.take(got, my_owner, axis=0)
    slab_size = rank * slab.shape[2]
    w_slabs = -(-w_part.size // slab_size)
    w_flat = jnp.pad(w_part.reshape(-1), (0, w_slabs * slab_size - w_part.size))
    buf = jnp.concatenate([slab, w_flat.reshape(w_slabs, rank, slab.shape[2])], axis=0)
    gathered = lax.all_gather(buf, "fsdp", axis=0, tiled=False)
    shares = gathered[:, :list_len]
    w_part_full = (
        gathered[:, list_len:]
        .reshape(fsdp_count, w_slabs * slab_size)[:, : w_part.size]
        .reshape(width, part_cols)
    )
    full_down = shares[..., :down_cols].transpose(1, 2, 0, 3).reshape(list_len, rank, width)
    full_up = shares[..., down_cols:].transpose(1, 2, 0, 3).reshape(list_len, rank, value_cols)

    up_x = [(i, (i + 2) % dp_count) for i in range(dp_count)]
    down_x = [(i, (i - 2) % dp_count) for i in range(dp_count)]
    from_left = lax.ppermute(w_part_full, "dp", up_x)
    from_right = lax.ppermute(w_part_full, "dp", down_x)
    half_part = part_cols // 2
    far_a = lax.ppermute(from_left[:, :half_part], "dp", up_x)
    far_b = lax.ppermute(from_right[:, half_part:], "dp", down_x)
    far = jnp.concatenate([far_a, far_b], axis=1)
    same_parity = [w_part_full, from_left, far, from_right]
    w_own = jnp.concatenate(same_parity, axis=1)
    w_partner = lax.ppermute(w_own, "dp", [(i, i ^ 1) for i in range(dp_count)])
    out_own = jnp.dot(tokens, w_own, preferred_element_type=f32)
    out_partner = jnp.dot(tokens, w_partner, preferred_element_type=f32)
    held = jnp.concatenate([out_own, out_partner], axis=1).reshape(tok_rows, dp_count, part_cols)
    part_ids = jnp.arange(dp_count, dtype=jnp.int32)
    partner_index = group_index ^ 1
    same = (part_ids % 2) == (group_index % 2)
    where_held = jnp.where(
        same,
        ((group_index - part_ids) % dp_count) // 2,
        dp_count // 2 + ((partner_index - part_ids) % dp_count) // 2,
    )
    frozen_rows = jnp.take(held, where_held, axis=1).reshape(tok_rows, value_cols)

    group_picks = window_composer_position[0]
    my_picks = lax.dynamic_slice_in_dim(group_picks, member_index * windows, windows, 0)
    slot_range = jnp.arange(list_len, dtype=jnp.int32)
    token_hot = jnp.broadcast_to(
        my_picks[:, None, None] == slot_range[None, None, :], (windows, WIN, list_len)
    ).reshape(tok_rows, list_len)
    hot_f = token_hot.astype(f32)

    down_flat = full_down.reshape(list_len * rank, width)
    up_flat = full_up.reshape(list_len * rank, value_cols)
    low_all = lax.dot_general(
        tokens, down_flat, (((1,), (1,)), ((), ())), preferred_element_type=f32
    ).reshape(tok_rows, list_len, rank)
    low = jnp.sum(low_all * hot_f[:, :, None], axis=1).astype(bf16)
    hot_h = token_hot.astype(bf16)
    masked_low = (hot_h[:, :, None] * low[:, None, :]).reshape(tok_rows, list_len * rank)
    adapter_change = jnp.dot(masked_low, up_flat, preferred_element_type=f32)
    value = (frozen_rows + ADAPTER_SCALE * adapter_change).astype(bf16)

    back_all = lax.dot_general(
        value_output_gradient, up_flat, (((1,), (1,)), ((), ())), preferred_element_type=f32
    ).reshape(tok_rows, list_len, rank)
    back = (ADAPTER_SCALE * jnp.sum(back_all * hot_f[:, :, None], axis=1)).astype(bf16)
    masked_back = (hot_h[:, :, None] * back[:, None, :]).reshape(tok_rows, list_len * rank)
    scaled_masked_low = masked_low * jnp.asarray(ADAPTER_SCALE, bf16)

    contract = (((0,), (0,)), ((), ()))
    part_down = lax.dot_general(masked_back, tokens, contract, preferred_element_type=f32)
    part_up = lax.dot_general(
        scaled_masked_low, value_output_gradient, contract, preferred_element_type=f32
    )
    rows = list_len * rank
    part_down = part_down.reshape(rows, fsdp_count, down_cols).transpose(1, 0, 2)
    part_up = part_up.reshape(rows, fsdp_count, up_cols).transpose(1, 0, 2)
    summed = lax.psum_scatter(
        jnp.concatenate([part_down, part_up], axis=2), "fsdp", scatter_dimension=0, tiled=True
    )[0]

    owner_range = jnp.arange(dp_count, dtype=jnp.int32)
    to_owner = my_owner[None, :] == owner_range[:, None]
    pick_index = jnp.sum(jnp.where(to_owner, slot_range[None, :], 0), axis=1)
    owner_has = jnp.any(to_owner, axis=1)
    send_grad = jnp.take(summed.reshape(list_len, rank, down_cols + up_cols), pick_index, axis=0)
    send_grad = jnp.where(owner_has[:, None, None], send_grad, 0.0)
    back_grad = lax.all_to_all(send_grad, "dp", split_axis=0, concat_axis=0, tiled=True)
    land = jnp.where(owned_any, locally_owned_slots, 0)
    arrived = jnp.where(owned_any[:, None, None], back_grad, 0.0)
    grad_down = jnp.zeros((each_owner_rows, rank, down_cols), f32).at[land].add(
        arrived[:, :, :down_cols]
    )
    grad_up = jnp.zeros((each_owner_rows, rank, up_cols), f32).at[land].add(
        arrived[:, :, down_cols:]
    )
    return (value, grad_down, grad_up)


def solution(mesh):
    return jax.shard_map(
        body,
        mesh=mesh,
        in_specs=(
            P(("dp", "fsdp"), None),
            P("fsdp", None),
            P("dp", None, "fsdp"),
            P("dp", None, "fsdp"),
            P(("dp", "fsdp"), None),
            P("dp", None),
            P(),
            P(),
        ),
        out_specs=(P(("dp", "fsdp"), None), P("dp", None, "fsdp"), P("dp", None, "fsdp")),
        check_vma=False,
    )
```

```python
import jax
import jax.numpy as jnp
from jax import lax
from jax.sharding import PartitionSpec as P

WIN = 128


ADAPTER_SCALE = 2.0


def body(
    tokens,
    frozen_value_matrix,
    adapter_down_maps,
    adapter_up_maps,
    value_output_gradient,
    window_composer_position,
    needed_composers,
    composer_storage_index,
):
    f32, bf16 = jnp.float32, jnp.bfloat16
    dp_count = lax.axis_size("dp")
    fsdp_count = lax.axis_size("fsdp")
    group_index = lax.axis_index("dp")
    member_index = lax.axis_index("fsdp")
    tok_rows, width = tokens.shape
    value_cols = frozen_value_matrix.shape[1]
    rank = adapter_down_maps.shape[1]
    each_owner_rows = adapter_down_maps.shape[0]
    down_cols = adapter_down_maps.shape[2]
    up_cols = adapter_up_maps.shape[2]
    list_len = needed_composers.shape[1]
    windows = tok_rows // WIN

    part_cols = value_cols // dp_count
    w_part = lax.dynamic_slice_in_dim(
        frozen_value_matrix, group_index * part_cols, part_cols, axis=1
    )
    w_part_full = lax.all_to_all(
        jnp.broadcast_to(w_part[None], (fsdp_count,) + w_part.shape), "fsdp", 0, 0, tiled=True
    ).reshape(width, part_cols)
    up_x = [(i, (i + 2) % dp_count) for i in range(dp_count)]
    down_x = [(i, (i - 2) % dp_count) for i in range(dp_count)]
    from_left = lax.ppermute(w_part_full, "dp", up_x)
    from_right = lax.ppermute(w_part_full, "dp", down_x)
    half_part = part_cols // 2
    far_a = lax.ppermute(from_left[:, :half_part], "dp", up_x)
    far_b = lax.ppermute(from_right[:, half_part:], "dp", down_x)
    far = jnp.concatenate([far_a, far_b], axis=1)
    same_parity = [w_part_full, from_left, far, from_right]
    w_own = jnp.concatenate(same_parity, axis=1)
    w_partner = lax.ppermute(w_own, "dp", [(i, i ^ 1) for i in range(dp_count)])
    out_own = jnp.dot(tokens, w_own, preferred_element_type=f32)
    out_partner = jnp.dot(tokens, w_partner, preferred_element_type=f32)
    held = jnp.concatenate([out_own, out_partner], axis=1).reshape(tok_rows, dp_count, part_cols)
    part_ids = jnp.arange(dp_count, dtype=jnp.int32)
    partner_index = group_index ^ 1
    same = (part_ids % 2) == (group_index % 2)
    where_held = jnp.where(
        same,
        ((group_index - part_ids) % dp_count) // 2,
        dp_count // 2 + ((partner_index - part_ids) % dp_count) // 2,
    )
    frozen_rows = jnp.take(held, where_held, axis=1).reshape(tok_rows, value_cols)

    list_slot = jnp.take(composer_storage_index, needed_composers, axis=0)
    list_owner = list_slot // each_owner_rows
    list_local = list_slot % each_owner_rows
    owned_here = list_owner == group_index
    locally_owned_slots = jnp.sum(jnp.where(owned_here, list_local, 0), axis=1)
    owned_any = jnp.any(owned_here, axis=1)
    send = jnp.concatenate(
        [
            jnp.take(adapter_down_maps, locally_owned_slots, axis=0),
            jnp.take(adapter_up_maps, locally_owned_slots, axis=0),
        ],
        axis=2,
    )
    send = jnp.where(owned_any[:, None, None], send, jnp.zeros((), send.dtype))
    got = lax.all_to_all(send, "dp", split_axis=0, concat_axis=0, tiled=True)
    my_owner = lax.dynamic_index_in_dim(list_owner, group_index, 0, keepdims=False)
    slab = jnp.take(got, my_owner, axis=0)
    shares = lax.all_gather(slab, "fsdp", axis=0, tiled=False)
    full_down = shares[..., :down_cols].transpose(1, 2, 0, 3).reshape(list_len, rank, width)
    full_up = shares[..., down_cols:].transpose(1, 2, 0, 3).reshape(list_len, rank, value_cols)

    group_picks = window_composer_position[0]
    my_picks = lax.dynamic_slice_in_dim(group_picks, member_index * windows, windows, 0)
    slot_range = jnp.arange(list_len, dtype=jnp.int32)
    token_hot = jnp.broadcast_to(
        my_picks[:, None, None] == slot_range[None, None, :], (windows, WIN, list_len)
    ).reshape(tok_rows, list_len)
    hot_f = token_hot.astype(f32)

    down_flat = full_down.reshape(list_len * rank, width)
    up_flat = full_up.reshape(list_len * rank, value_cols)
    low_all = lax.dot_general(
        tokens, down_flat, (((1,), (1,)), ((), ())), preferred_element_type=f32
    ).reshape(tok_rows, list_len, rank)
    low = jnp.sum(low_all * hot_f[:, :, None], axis=1).astype(bf16)
    hot_h = token_hot.astype(bf16)
    masked_low = (hot_h[:, :, None] * low[:, None, :]).reshape(tok_rows, list_len * rank)
    adapter_change = jnp.dot(masked_low, up_flat, preferred_element_type=f32)
    value = (frozen_rows + ADAPTER_SCALE * adapter_change).astype(bf16)

    back_all = lax.dot_general(
        value_output_gradient, up_flat, (((1,), (1,)), ((), ())), preferred_element_type=f32
    ).reshape(tok_rows, list_len, rank)
    back = (ADAPTER_SCALE * jnp.sum(back_all * hot_f[:, :, None], axis=1)).astype(bf16)
    masked_back = (hot_h[:, :, None] * back[:, None, :]).reshape(tok_rows, list_len * rank)
    scaled_masked_low = masked_low * jnp.asarray(ADAPTER_SCALE, bf16)

    contract = (((0,), (0,)), ((), ()))
    part_down = lax.dot_general(masked_back, tokens, contract, preferred_element_type=f32)
    part_up = lax.dot_general(
        scaled_masked_low, value_output_gradient, contract, preferred_element_type=f32
    )
    rows = list_len * rank
    part_down = part_down.reshape(rows, fsdp_count, down_cols).transpose(1, 0, 2)
    part_up = part_up.reshape(rows, fsdp_count, up_cols).transpose(1, 0, 2)
    summed = lax.psum_scatter(
        jnp.concatenate([part_down, part_up], axis=2), "fsdp", scatter_dimension=0, tiled=True
    )[0]

    owner_range = jnp.arange(dp_count, dtype=jnp.int32)
    to_owner = my_owner[None, :] == owner_range[:, None]
    pick_index = jnp.sum(jnp.where(to_owner, slot_range[None, :], 0), axis=1)
    owner_has = jnp.any(to_owner, axis=1)
    send_grad = jnp.take(summed.reshape(list_len, rank, down_cols + up_cols), pick_index, axis=0)
    send_grad = jnp.where(owner_has[:, None, None], send_grad, 0.0)
    back_grad = lax.all_to_all(send_grad, "dp", split_axis=0, concat_axis=0, tiled=True)
    land = jnp.where(owned_any, locally_owned_slots, 0)
    arrived = jnp.where(owned_any[:, None, None], back_grad, 0.0)
    grad_down = jnp.zeros((each_owner_rows, rank, down_cols), f32).at[land].add(
        arrived[:, :, :down_cols]
    )
    grad_up = jnp.zeros((each_owner_rows, rank, up_cols), f32).at[land].add(
        arrived[:, :, down_cols:]
    )
    return (value, grad_down, grad_up)


def solution(mesh):
    return jax.shard_map(
        body,
        mesh=mesh,
        in_specs=(
            P(("dp", "fsdp"), None),
            P("fsdp", None),
            P("dp", None, "fsdp"),
            P("dp", None, "fsdp"),
            P(("dp", "fsdp"), None),
            P("dp", None),
            P(),
            P(),
        ),
        out_specs=(P(("dp", "fsdp"), None), P("dp", None, "fsdp"), P("dp", None, "fsdp")),
        check_vma=False,
    )
```

```python
import jax
import jax.numpy as jnp
from jax import lax
from jax.sharding import PartitionSpec as P

WIN = 128


ADAPTER_SCALE = 2.0


def body(
    tokens,
    frozen_value_matrix,
    adapter_down_maps,
    adapter_up_maps,
    value_output_gradient,
    window_composer_position,
    needed_composers,
    composer_storage_index,
):
    f32, bf16 = jnp.float32, jnp.bfloat16
    dp_count = lax.axis_size("dp")
    fsdp_count = lax.axis_size("fsdp")
    group_index = lax.axis_index("dp")
    member_index = lax.axis_index("fsdp")
    tok_rows, width = tokens.shape
    value_cols = frozen_value_matrix.shape[1]
    rank = adapter_down_maps.shape[1]
    each_owner_rows = adapter_down_maps.shape[0]
    down_cols = adapter_down_maps.shape[2]
    up_cols = adapter_up_maps.shape[2]
    list_len = needed_composers.shape[1]
    windows = tok_rows // WIN

    part_cols = value_cols // dp_count
    w_part = lax.dynamic_slice_in_dim(
        frozen_value_matrix, group_index * part_cols, part_cols, axis=1
    )
    nz = 4 if fsdp_count % 4 == 0 else 1
    ny = fsdp_count // nz
    fz, fy = member_index % nz, member_index // nz

    def shift(dy, dz):
        return [
            (j, ((j // nz + dy) % ny) * nz + (j % nz + dz) % nz) for j in range(fsdp_count)
        ]

    zs = [w_part] + [lax.ppermute(w_part, "fsdp", shift(0, t)) for t in range(1, nz)]
    z_sorted = jnp.take(jnp.stack(zs), (fz - jnp.arange(nz)) % nz, axis=0)
    ys = [z_sorted] + [lax.ppermute(z_sorted, "fsdp", shift(t, 0)) for t in range(1, ny)]
    w_part_full = jnp.take(jnp.stack(ys), (fy - jnp.arange(ny)) % ny, axis=0).reshape(
        width, part_cols
    )
    up_x = [(i, (i + 2) % dp_count) for i in range(dp_count)]
    down_x = [(i, (i - 2) % dp_count) for i in range(dp_count)]
    from_left = lax.ppermute(w_part_full, "dp", up_x)
    from_right = lax.ppermute(w_part_full, "dp", down_x)
    half_part = part_cols // 2
    far_a = lax.ppermute(from_left[:, :half_part], "dp", up_x)
    far_b = lax.ppermute(from_right[:, half_part:], "dp", down_x)
    far = jnp.concatenate([far_a, far_b], axis=1)
    same_parity = [w_part_full, from_left, far, from_right]
    w_own = jnp.concatenate(same_parity, axis=1)
    w_partner = lax.ppermute(w_own, "dp", [(i, i ^ 1) for i in range(dp_count)])
    out_own = jnp.dot(tokens, w_own, preferred_element_type=f32)
    out_partner = jnp.dot(tokens, w_partner, preferred_element_type=f32)
    held = jnp.concatenate([out_own, out_partner], axis=1).reshape(tok_rows, dp_count, part_cols)
    part_ids = jnp.arange(dp_count, dtype=jnp.int32)
    partner_index = group_index ^ 1
    same = (part_ids % 2) == (group_index % 2)
    where_held = jnp.where(
        same,
        ((group_index - part_ids) % dp_count) // 2,
        dp_count // 2 + ((partner_index - part_ids) % dp_count) // 2,
    )
    frozen_rows = jnp.take(held, where_held, axis=1).reshape(tok_rows, value_cols)

    list_slot = jnp.take(composer_storage_index, needed_composers, axis=0)
    list_owner = list_slot // each_owner_rows
    list_local = list_slot % each_owner_rows
    owned_here = list_owner == group_index
    locally_owned_slots = jnp.sum(jnp.where(owned_here, list_local, 0), axis=1)
    owned_any = jnp.any(owned_here, axis=1)
    send = jnp.concatenate(
        [
            jnp.take(adapter_down_maps, locally_owned_slots, axis=0),
            jnp.take(adapter_up_maps, locally_owned_slots, axis=0),
        ],
        axis=2,
    )
    send = jnp.where(owned_any[:, None, None], send, jnp.zeros((), send.dtype))
    got = lax.all_to_all(send, "dp", split_axis=0, concat_axis=0, tiled=True)
    my_owner = lax.dynamic_index_in_dim(list_owner, group_index, 0, keepdims=False)
    slab = jnp.take(got, my_owner, axis=0)
    w_part_full, slab = lax.optimization_barrier((w_part_full, slab))
    shares = lax.all_gather(slab, "fsdp", axis=0, tiled=False)
    shares, from_left, from_right = lax.optimization_barrier((shares, from_left, from_right))
    full_down = shares[..., :down_cols].transpose(1, 2, 0, 3).reshape(list_len, rank, width)
    full_up = shares[..., down_cols:].transpose(1, 2, 0, 3).reshape(list_len, rank, value_cols)

    group_picks = window_composer_position[0]
    my_picks = lax.dynamic_slice_in_dim(group_picks, member_index * windows, windows, 0)
    slot_range = jnp.arange(list_len, dtype=jnp.int32)
    token_hot = jnp.broadcast_to(
        my_picks[:, None, None] == slot_range[None, None, :], (windows, WIN, list_len)
    ).reshape(tok_rows, list_len)
    hot_f = token_hot.astype(f32)

    down_flat = full_down.reshape(list_len * rank, width)
    up_flat = full_up.reshape(list_len * rank, value_cols)
    low_all = lax.dot_general(
        tokens, down_flat, (((1,), (1,)), ((), ())), preferred_element_type=f32
    ).reshape(tok_rows, list_len, rank)
    low = jnp.sum(low_all * hot_f[:, :, None], axis=1).astype(bf16)
    hot_h = token_hot.astype(bf16)
    masked_low = (hot_h[:, :, None] * low[:, None, :]).reshape(tok_rows, list_len * rank)
    adapter_change = jnp.dot(masked_low, up_flat, preferred_element_type=f32)
    value = (frozen_rows + ADAPTER_SCALE * adapter_change).astype(bf16)

    back_all = lax.dot_general(
        value_output_gradient, up_flat, (((1,), (1,)), ((), ())), preferred_element_type=f32
    ).reshape(tok_rows, list_len, rank)
    back = (ADAPTER_SCALE * jnp.sum(back_all * hot_f[:, :, None], axis=1)).astype(bf16)
    masked_back = (hot_h[:, :, None] * back[:, None, :]).reshape(tok_rows, list_len * rank)
    scaled_masked_low = masked_low * jnp.asarray(ADAPTER_SCALE, bf16)

    contract = (((0,), (0,)), ((), ()))
    part_down = lax.dot_general(masked_back, tokens, contract, preferred_element_type=f32)
    part_up = lax.dot_general(
        scaled_masked_low, value_output_gradient, contract, preferred_element_type=f32
    )
    rows = list_len * rank
    part_down = part_down.reshape(rows, fsdp_count, down_cols).transpose(1, 0, 2)
    part_up = part_up.reshape(rows, fsdp_count, up_cols).transpose(1, 0, 2)
    summed = lax.psum_scatter(
        jnp.concatenate([part_down, part_up], axis=2), "fsdp", scatter_dimension=0, tiled=True
    )[0]

    owner_range = jnp.arange(dp_count, dtype=jnp.int32)
    to_owner = my_owner[None, :] == owner_range[:, None]
    pick_index = jnp.sum(jnp.where(to_owner, slot_range[None, :], 0), axis=1)
    owner_has = jnp.any(to_owner, axis=1)
    send_grad = jnp.take(summed.reshape(list_len, rank, down_cols + up_cols), pick_index, axis=0)
    send_grad = jnp.where(owner_has[:, None, None], send_grad, 0.0)
    back_grad = lax.all_to_all(send_grad, "dp", split_axis=0, concat_axis=0, tiled=True)
    land = jnp.where(owned_any, locally_owned_slots, 0)
    arrived = jnp.where(owned_any[:, None, None], back_grad, 0.0)
    grad_down = jnp.zeros((each_owner_rows, rank, down_cols), f32).at[land].add(
        arrived[:, :, :down_cols]
    )
    grad_up = jnp.zeros((each_owner_rows, rank, up_cols), f32).at[land].add(
        arrived[:, :, down_cols:]
    )
    return (value, grad_down, grad_up)


def solution(mesh):
    return jax.shard_map(
        body,
        mesh=mesh,
        in_specs=(
            P(("dp", "fsdp"), None),
            P("fsdp", None),
            P("dp", None, "fsdp"),
            P("dp", None, "fsdp"),
            P(("dp", "fsdp"), None),
            P("dp", None),
            P(),
            P(),
        ),
        out_specs=(P(("dp", "fsdp"), None), P("dp", None, "fsdp"), P("dp", None, "fsdp")),
        check_vma=False,
    )
```

```python
import jax
import jax.numpy as jnp
from jax import lax
from jax.sharding import PartitionSpec as P

WIN = 128


ADAPTER_SCALE = 2.0


def body(
    tokens,
    frozen_value_matrix,
    adapter_down_maps,
    adapter_up_maps,
    value_output_gradient,
    window_composer_position,
    needed_composers,
    composer_storage_index,
):
    f32, bf16 = jnp.float32, jnp.bfloat16
    dp_count = lax.axis_size("dp")
    fsdp_count = lax.axis_size("fsdp")
    group_index = lax.axis_index("dp")
    member_index = lax.axis_index("fsdp")
    tok_rows, width = tokens.shape
    value_cols = frozen_value_matrix.shape[1]
    rank = adapter_down_maps.shape[1]
    each_owner_rows = adapter_down_maps.shape[0]
    down_cols = adapter_down_maps.shape[2]
    up_cols = adapter_up_maps.shape[2]
    list_len = needed_composers.shape[1]
    windows = tok_rows // WIN

    part_cols = value_cols // dp_count
    w_part = lax.dynamic_slice_in_dim(
        frozen_value_matrix, group_index * part_cols, part_cols, axis=1
    )
    nz = 4 if fsdp_count % 4 == 0 else 1
    ny = fsdp_count // nz
    fz, fy = member_index % nz, member_index // nz

    def shift(dy, dz):
        return [
            (j, ((j // nz + dy) % ny) * nz + (j % nz + dz) % nz) for j in range(fsdp_count)
        ]

    zs = [w_part] + [lax.ppermute(w_part, "fsdp", shift(0, t)) for t in range(1, nz)]
    z_sorted = jnp.take(jnp.stack(zs), (fz - jnp.arange(nz)) % nz, axis=0)
    ys = [z_sorted] + [lax.ppermute(z_sorted, "fsdp", shift(t, 0)) for t in range(1, ny)]
    w_part_full = jnp.take(jnp.stack(ys), (fy - jnp.arange(ny)) % ny, axis=0).reshape(
        width, part_cols
    )
    list_slot = jnp.take(composer_storage_index, needed_composers, axis=0)
    list_owner = list_slot // each_owner_rows
    list_local = list_slot % each_owner_rows
    owned_here = list_owner == group_index
    locally_owned_slots = jnp.sum(jnp.where(owned_here, list_local, 0), axis=1)
    owned_any = jnp.any(owned_here, axis=1)
    send = jnp.concatenate(
        [
            jnp.take(adapter_down_maps, locally_owned_slots, axis=0),
            jnp.take(adapter_up_maps, locally_owned_slots, axis=0),
        ],
        axis=2,
    )
    send = jnp.where(owned_any[:, None, None], send, jnp.zeros((), send.dtype))
    got = lax.all_to_all(send, "dp", split_axis=0, concat_axis=0, tiled=True)
    my_owner = lax.dynamic_index_in_dim(list_owner, group_index, 0, keepdims=False)
    slab = jnp.take(got, my_owner, axis=0)
    shares = lax.all_gather(slab, "fsdp", axis=0, tiled=False)
    shares, w_part_ready = lax.optimization_barrier((shares, w_part_full))
    full_down = shares[..., :down_cols].transpose(1, 2, 0, 3).reshape(list_len, rank, width)
    full_up = shares[..., down_cols:].transpose(1, 2, 0, 3).reshape(list_len, rank, value_cols)

    up_x = [(i, (i + 2) % dp_count) for i in range(dp_count)]
    down_x = [(i, (i - 2) % dp_count) for i in range(dp_count)]
    from_left = lax.ppermute(w_part_ready, "dp", up_x)
    from_right = lax.ppermute(w_part_ready, "dp", down_x)
    half_part = part_cols // 2
    far_a = lax.ppermute(from_left[:, :half_part], "dp", up_x)
    far_b = lax.ppermute(from_right[:, half_part:], "dp", down_x)
    far = jnp.concatenate([far_a, far_b], axis=1)
    same_parity = [w_part_ready, from_left, far, from_right]
    w_own = jnp.concatenate(same_parity, axis=1)
    w_partner = lax.ppermute(w_own, "dp", [(i, i ^ 1) for i in range(dp_count)])
    out_own = jnp.dot(tokens, w_own, preferred_element_type=f32)
    out_partner = jnp.dot(tokens, w_partner, preferred_element_type=f32)
    held = jnp.concatenate([out_own, out_partner], axis=1).reshape(tok_rows, dp_count, part_cols)
    part_ids = jnp.arange(dp_count, dtype=jnp.int32)
    partner_index = group_index ^ 1
    same = (part_ids % 2) == (group_index % 2)
    where_held = jnp.where(
        same,
        ((group_index - part_ids) % dp_count) // 2,
        dp_count // 2 + ((partner_index - part_ids) % dp_count) // 2,
    )
    frozen_rows = jnp.take(held, where_held, axis=1).reshape(tok_rows, value_cols)

    group_picks = window_composer_position[0]
    my_picks = lax.dynamic_slice_in_dim(group_picks, member_index * windows, windows, 0)
    slot_range = jnp.arange(list_len, dtype=jnp.int32)
    token_hot = jnp.broadcast_to(
        my_picks[:, None, None] == slot_range[None, None, :], (windows, WIN, list_len)
    ).reshape(tok_rows, list_len)
    hot_f = token_hot.astype(f32)

    down_flat = full_down.reshape(list_len * rank, width)
    up_flat = full_up.reshape(list_len * rank, value_cols)
    low_all = lax.dot_general(
        tokens, down_flat, (((1,), (1,)), ((), ())), preferred_element_type=f32
    ).reshape(tok_rows, list_len, rank)
    low = jnp.sum(low_all * hot_f[:, :, None], axis=1).astype(bf16)
    hot_h = token_hot.astype(bf16)
    masked_low = (hot_h[:, :, None] * low[:, None, :]).reshape(tok_rows, list_len * rank)
    adapter_change = jnp.dot(masked_low, up_flat, preferred_element_type=f32)
    value = (frozen_rows + ADAPTER_SCALE * adapter_change).astype(bf16)

    back_all = lax.dot_general(
        value_output_gradient, up_flat, (((1,), (1,)), ((), ())), preferred_element_type=f32
    ).reshape(tok_rows, list_len, rank)
    back = (ADAPTER_SCALE * jnp.sum(back_all * hot_f[:, :, None], axis=1)).astype(bf16)
    masked_back = (hot_h[:, :, None] * back[:, None, :]).reshape(tok_rows, list_len * rank)
    scaled_masked_low = masked_low * jnp.asarray(ADAPTER_SCALE, bf16)

    contract = (((0,), (0,)), ((), ()))
    part_down = lax.dot_general(masked_back, tokens, contract, preferred_element_type=f32)
    part_up = lax.dot_general(
        scaled_masked_low, value_output_gradient, contract, preferred_element_type=f32
    )
    rows = list_len * rank
    part_down = part_down.reshape(rows, fsdp_count, down_cols).transpose(1, 0, 2)
    part_up = part_up.reshape(rows, fsdp_count, up_cols).transpose(1, 0, 2)
    summed = lax.psum_scatter(
        jnp.concatenate([part_down, part_up], axis=2), "fsdp", scatter_dimension=0, tiled=True
    )[0]

    owner_range = jnp.arange(dp_count, dtype=jnp.int32)
    to_owner = my_owner[None, :] == owner_range[:, None]
    pick_index = jnp.sum(jnp.where(to_owner, slot_range[None, :], 0), axis=1)
    owner_has = jnp.any(to_owner, axis=1)
    send_grad = jnp.take(summed.reshape(list_len, rank, down_cols + up_cols), pick_index, axis=0)
    send_grad = jnp.where(owner_has[:, None, None], send_grad, 0.0)
    back_grad = lax.all_to_all(send_grad, "dp", split_axis=0, concat_axis=0, tiled=True)
    land = jnp.where(owned_any, locally_owned_slots, 0)
    arrived = jnp.where(owned_any[:, None, None], back_grad, 0.0)
    grad_down = jnp.zeros((each_owner_rows, rank, down_cols), f32).at[land].add(
        arrived[:, :, :down_cols]
    )
    grad_up = jnp.zeros((each_owner_rows, rank, up_cols), f32).at[land].add(
        arrived[:, :, down_cols:]
    )
    return (value, grad_down, grad_up)


def solution(mesh):
    return jax.shard_map(
        body,
        mesh=mesh,
        in_specs=(
            P(("dp", "fsdp"), None),
            P("fsdp", None),
            P("dp", None, "fsdp"),
            P("dp", None, "fsdp"),
            P(("dp", "fsdp"), None),
            P("dp", None),
            P(),
            P(),
        ),
        out_specs=(P(("dp", "fsdp"), None), P("dp", None, "fsdp"), P("dp", None, "fsdp")),
        check_vma=False,
    )
```

```python
import jax
import jax.numpy as jnp
from jax import lax
from jax.sharding import PartitionSpec as P

WIN = 128


ADAPTER_SCALE = 2.0


def body(
    tokens,
    frozen_value_matrix,
    adapter_down_maps,
    adapter_up_maps,
    value_output_gradient,
    window_composer_position,
    needed_composers,
    composer_storage_index,
):
    f32, bf16 = jnp.float32, jnp.bfloat16
    dp_count = lax.axis_size("dp")
    fsdp_count = lax.axis_size("fsdp")
    group_index = lax.axis_index("dp")
    member_index = lax.axis_index("fsdp")
    tok_rows, width = tokens.shape
    value_cols = frozen_value_matrix.shape[1]
    rank = adapter_down_maps.shape[1]
    each_owner_rows = adapter_down_maps.shape[0]
    down_cols = adapter_down_maps.shape[2]
    up_cols = adapter_up_maps.shape[2]
    list_len = needed_composers.shape[1]
    windows = tok_rows // WIN

    part_cols = value_cols // dp_count
    w_part = lax.dynamic_slice_in_dim(
        frozen_value_matrix, group_index * part_cols, part_cols, axis=1
    )
    w_part_full = lax.all_gather(w_part, "fsdp", axis=0, tiled=True)
    up_x = [(i, (i + 2) % dp_count) for i in range(dp_count)]
    down_x = [(i, (i - 2) % dp_count) for i in range(dp_count)]
    from_left = lax.ppermute(w_part_full, "dp", up_x)
    from_right = lax.ppermute(w_part_full, "dp", down_x)
    half_part = part_cols // 2
    far_a = lax.ppermute(from_left[:, :half_part], "dp", up_x)
    far_b = lax.ppermute(from_right[:, half_part:], "dp", down_x)
    far = jnp.concatenate([far_a, far_b], axis=1)
    same_parity = [w_part_full, from_left, far, from_right]
    w_own = jnp.concatenate(same_parity, axis=1)
    w_partner = lax.ppermute(w_own, "dp", [(i, i ^ 1) for i in range(dp_count)])
    out_own = jnp.dot(tokens, w_own, preferred_element_type=f32)
    out_partner = jnp.dot(tokens, w_partner, preferred_element_type=f32)
    held = jnp.concatenate([out_own, out_partner], axis=1).reshape(tok_rows, dp_count, part_cols)
    part_ids = jnp.arange(dp_count, dtype=jnp.int32)
    partner_index = group_index ^ 1
    same = (part_ids % 2) == (group_index % 2)
    where_held = jnp.where(
        same,
        ((group_index - part_ids) % dp_count) // 2,
        dp_count // 2 + ((partner_index - part_ids) % dp_count) // 2,
    )
    frozen_rows = jnp.take(held, where_held, axis=1).reshape(tok_rows, value_cols)

    list_slot = jnp.take(composer_storage_index, needed_composers, axis=0)
    list_owner = list_slot // each_owner_rows
    list_local = list_slot % each_owner_rows
    owned_here = list_owner == group_index
    locally_owned_slots = jnp.sum(jnp.where(owned_here, list_local, 0), axis=1)
    owned_any = jnp.any(owned_here, axis=1)
    send = jnp.concatenate(
        [
            jnp.take(adapter_down_maps, locally_owned_slots, axis=0),
            jnp.take(adapter_up_maps, locally_owned_slots, axis=0),
        ],
        axis=2,
    )
    send = jnp.where(owned_any[:, None, None], send, jnp.zeros((), send.dtype))
    got = lax.all_to_all(send, "dp", split_axis=0, concat_axis=0, tiled=True)
    my_owner = lax.dynamic_index_in_dim(list_owner, group_index, 0, keepdims=False)
    slab = jnp.take(got, my_owner, axis=0)
    shares = lax.all_gather(slab, "fsdp", axis=0, tiled=False)
    full_down = shares[..., :down_cols].transpose(1, 2, 0, 3).reshape(list_len, rank, width)
    full_up = shares[..., down_cols:].transpose(1, 2, 0, 3).reshape(list_len, rank, value_cols)

    group_picks = window_composer_position[0]
    my_picks = lax.dynamic_slice_in_dim(group_picks, member_index * windows, windows, 0)
    slot_range = jnp.arange(list_len, dtype=jnp.int32)
    token_hot = jnp.broadcast_to(
        my_picks[:, None, None] == slot_range[None, None, :], (windows, WIN, list_len)
    ).reshape(tok_rows, list_len)
    hot_f = token_hot.astype(f32)

    down_flat = full_down.reshape(list_len * rank, width)
    up_flat = full_up.reshape(list_len * rank, value_cols)
    low_all = lax.dot_general(
        tokens, down_flat, (((1,), (1,)), ((), ())), preferred_element_type=f32
    ).reshape(tok_rows, list_len, rank)
    low = jnp.sum(low_all * hot_f[:, :, None], axis=1).astype(bf16)
    hot_h = token_hot.astype(bf16)
    masked_low = (hot_h[:, :, None] * low[:, None, :]).reshape(tok_rows, list_len * rank)
    adapter_change = jnp.dot(masked_low, up_flat, preferred_element_type=f32)
    value = (frozen_rows + ADAPTER_SCALE * adapter_change).astype(bf16)

    back_all = lax.dot_general(
        value_output_gradient, up_flat, (((1,), (1,)), ((), ())), preferred_element_type=f32
    ).reshape(tok_rows, list_len, rank)
    back = (ADAPTER_SCALE * jnp.sum(back_all * hot_f[:, :, None], axis=1)).astype(bf16)
    masked_back = (hot_h[:, :, None] * back[:, None, :]).reshape(tok_rows, list_len * rank)
    scaled_masked_low = masked_low * jnp.asarray(ADAPTER_SCALE, bf16)

    contract = (((0,), (0,)), ((), ()))
    part_down = lax.dot_general(masked_back, tokens, contract, preferred_element_type=f32)
    part_up = lax.dot_general(
        scaled_masked_low, value_output_gradient, contract, preferred_element_type=f32
    )
    rows = list_len * rank
    part_down = part_down.reshape(rows, fsdp_count, down_cols).transpose(1, 0, 2)
    part_up = part_up.reshape(rows, fsdp_count, up_cols).transpose(1, 0, 2)
    summed = lax.psum_scatter(
        jnp.concatenate([part_down, part_up], axis=2), "fsdp", scatter_dimension=0, tiled=True
    )[0]

    owner_range = jnp.arange(dp_count, dtype=jnp.int32)
    to_owner = my_owner[None, :] == owner_range[:, None]
    pick_index = jnp.sum(jnp.where(to_owner, slot_range[None, :], 0), axis=1)
    owner_has = jnp.any(to_owner, axis=1)
    send_grad = jnp.take(summed.reshape(list_len, rank, down_cols + up_cols), pick_index, axis=0)
    send_grad = jnp.where(owner_has[:, None, None], send_grad, 0.0)
    back_grad = lax.all_to_all(send_grad, "dp", split_axis=0, concat_axis=0, tiled=True)
    land = jnp.where(owned_any, locally_owned_slots, 0)
    arrived = back_grad
    grad_down = jnp.zeros((each_owner_rows, rank, down_cols), f32).at[land].add(
        arrived[:, :, :down_cols]
    )
    grad_up = jnp.zeros((each_owner_rows, rank, up_cols), f32).at[land].add(
        arrived[:, :, down_cols:]
    )
    return (value, grad_down, grad_up)


def solution(mesh):
    return jax.shard_map(
        body,
        mesh=mesh,
        in_specs=(
            P(("dp", "fsdp"), None),
            P("fsdp", None),
            P("dp", None, "fsdp"),
            P("dp", None, "fsdp"),
            P(("dp", "fsdp"), None),
            P("dp", None),
            P(),
            P(),
        ),
        out_specs=(P(("dp", "fsdp"), None), P("dp", None, "fsdp"), P("dp", None, "fsdp")),
        check_vma=False,
    )
```

```python
import jax
import jax.numpy as jnp
from jax import lax
from jax.sharding import PartitionSpec as P

WIN = 128


ADAPTER_SCALE = 2.0


def body(
    tokens,
    frozen_value_matrix,
    adapter_down_maps,
    adapter_up_maps,
    value_output_gradient,
    window_composer_position,
    needed_composers,
    composer_storage_index,
):
    f32, bf16 = jnp.float32, jnp.bfloat16
    dp_count = lax.axis_size("dp")
    fsdp_count = lax.axis_size("fsdp")
    group_index = lax.axis_index("dp")
    member_index = lax.axis_index("fsdp")
    tok_rows, width = tokens.shape
    value_cols = frozen_value_matrix.shape[1]
    rank = adapter_down_maps.shape[1]
    each_owner_rows = adapter_down_maps.shape[0]
    down_cols = adapter_down_maps.shape[2]
    up_cols = adapter_up_maps.shape[2]
    list_len = needed_composers.shape[1]
    windows = tok_rows // WIN

    part_cols = value_cols // dp_count
    w_part = lax.dynamic_slice_in_dim(
        frozen_value_matrix, group_index * part_cols, part_cols, axis=1
    )
    w_part_full = lax.all_gather(w_part, "fsdp", axis=0, tiled=True)
    up_x = [(i, (i + 2) % dp_count) for i in range(dp_count)]
    down_x = [(i, (i - 2) % dp_count) for i in range(dp_count)]
    from_left = lax.ppermute(w_part_full, "dp", up_x)
    from_right = lax.ppermute(w_part_full, "dp", down_x)
    half_part = part_cols // 2
    far_a = lax.ppermute(from_left[:, :half_part], "dp", up_x)
    far_b = lax.ppermute(from_right[:, half_part:], "dp", down_x)
    far = jnp.concatenate([far_a, far_b], axis=1)
    same_parity = [w_part_full, from_left, far, from_right]
    w_own = jnp.concatenate(same_parity, axis=1)
    w_partner = lax.ppermute(w_own, "dp", [(i, i ^ 1) for i in range(dp_count)])
    out_own = jnp.dot(tokens, w_own, preferred_element_type=f32)
    out_partner = jnp.dot(tokens, w_partner, preferred_element_type=f32)
    held = jnp.concatenate([out_own, out_partner], axis=1).reshape(tok_rows, dp_count, part_cols)
    part_ids = jnp.arange(dp_count, dtype=jnp.int32)
    partner_index = group_index ^ 1
    same = (part_ids % 2) == (group_index % 2)
    where_held = jnp.where(
        same,
        ((group_index - part_ids) % dp_count) // 2,
        dp_count // 2 + ((partner_index - part_ids) % dp_count) // 2,
    )
    frozen_rows = jnp.take(held, where_held, axis=1).reshape(tok_rows, value_cols)

    list_slot = jnp.take(composer_storage_index, needed_composers, axis=0)
    list_owner = list_slot // each_owner_rows
    list_local = list_slot % each_owner_rows
    owned_here = list_owner == group_index
    locally_owned_slots = jnp.sum(jnp.where(owned_here, list_local, 0), axis=1)
    owned_any = jnp.any(owned_here, axis=1)
    pick = (
        (locally_owned_slots[:, None] == jnp.arange(each_owner_rows, dtype=jnp.int32)[None, :])
        & owned_any[:, None]
    ).astype(adapter_down_maps.dtype)
    send = jnp.concatenate(
        [
            jnp.einsum("sk,krd->srd", pick, adapter_down_maps, preferred_element_type=f32),
            jnp.einsum("sk,krd->srd", pick, adapter_up_maps, preferred_element_type=f32),
        ],
        axis=2,
    ).astype(adapter_down_maps.dtype)
    got = lax.all_to_all(send, "dp", split_axis=0, concat_axis=0, tiled=True)
    my_owner = lax.dynamic_index_in_dim(list_owner, group_index, 0, keepdims=False)
    slab = jnp.take(got, my_owner, axis=0)
    shares = lax.all_gather(slab, "fsdp", axis=0, tiled=False)
    full_down = shares[..., :down_cols].transpose(1, 2, 0, 3).reshape(list_len, rank, width)
    full_up = shares[..., down_cols:].transpose(1, 2, 0, 3).reshape(list_len, rank, value_cols)

    group_picks = window_composer_position[0]
    my_picks = lax.dynamic_slice_in_dim(group_picks, member_index * windows, windows, 0)
    slot_range = jnp.arange(list_len, dtype=jnp.int32)
    token_hot = jnp.broadcast_to(
        my_picks[:, None, None] == slot_range[None, None, :], (windows, WIN, list_len)
    ).reshape(tok_rows, list_len)
    hot_f = token_hot.astype(f32)

    down_flat = full_down.reshape(list_len * rank, width)
    up_flat = full_up.reshape(list_len * rank, value_cols)
    low_all = lax.dot_general(
        tokens, down_flat, (((1,), (1,)), ((), ())), preferred_element_type=f32
    ).reshape(tok_rows, list_len, rank)
    low = jnp.sum(low_all * hot_f[:, :, None], axis=1).astype(bf16)
    hot_h = token_hot.astype(bf16)
    masked_low = (hot_h[:, :, None] * low[:, None, :]).reshape(tok_rows, list_len * rank)
    adapter_change = jnp.dot(masked_low, up_flat, preferred_element_type=f32)
    value = (frozen_rows + ADAPTER_SCALE * adapter_change).astype(bf16)

    back_all = lax.dot_general(
        value_output_gradient, up_flat, (((1,), (1,)), ((), ())), preferred_element_type=f32
    ).reshape(tok_rows, list_len, rank)
    back = (ADAPTER_SCALE * jnp.sum(back_all * hot_f[:, :, None], axis=1)).astype(bf16)
    masked_back = (hot_h[:, :, None] * back[:, None, :]).reshape(tok_rows, list_len * rank)
    scaled_masked_low = masked_low * jnp.asarray(ADAPTER_SCALE, bf16)

    contract = (((0,), (0,)), ((), ()))
    part_down = lax.dot_general(masked_back, tokens, contract, preferred_element_type=f32)
    part_up = lax.dot_general(
        scaled_masked_low, value_output_gradient, contract, preferred_element_type=f32
    )
    rows = list_len * rank
    part_down = part_down.reshape(rows, fsdp_count, down_cols).transpose(1, 0, 2)
    part_up = part_up.reshape(rows, fsdp_count, up_cols).transpose(1, 0, 2)
    summed = lax.psum_scatter(
        jnp.concatenate([part_down, part_up], axis=2), "fsdp", scatter_dimension=0, tiled=True
    )[0]

    owner_range = jnp.arange(dp_count, dtype=jnp.int32)
    to_owner = my_owner[None, :] == owner_range[:, None]
    pick_index = jnp.sum(jnp.where(to_owner, slot_range[None, :], 0), axis=1)
    owner_has = jnp.any(to_owner, axis=1)
    send_grad = jnp.take(summed.reshape(list_len, rank, down_cols + up_cols), pick_index, axis=0)
    send_grad = jnp.where(owner_has[:, None, None], send_grad, 0.0)
    back_grad = lax.all_to_all(send_grad, "dp", split_axis=0, concat_axis=0, tiled=True)
    land = jnp.where(owned_any, locally_owned_slots, 0)
    arrived = jnp.where(owned_any[:, None, None], back_grad, 0.0)
    grad_down = jnp.zeros((each_owner_rows, rank, down_cols), f32).at[land].add(
        arrived[:, :, :down_cols]
    )
    grad_up = jnp.zeros((each_owner_rows, rank, up_cols), f32).at[land].add(
        arrived[:, :, down_cols:]
    )
    return (value, grad_down, grad_up)


def solution(mesh):
    return jax.shard_map(
        body,
        mesh=mesh,
        in_specs=(
            P(("dp", "fsdp"), None),
            P("fsdp", None),
            P("dp", None, "fsdp"),
            P("dp", None, "fsdp"),
            P(("dp", "fsdp"), None),
            P("dp", None),
            P(),
            P(),
        ),
        out_specs=(P(("dp", "fsdp"), None), P("dp", None, "fsdp"), P("dp", None, "fsdp")),
        check_vma=False,
    )
```

```python
import jax
import jax.numpy as jnp
from jax import lax
from jax.sharding import PartitionSpec as P

WIN = 128


ADAPTER_SCALE = 2.0


def body(
    tokens,
    frozen_value_matrix,
    adapter_down_maps,
    adapter_up_maps,
    value_output_gradient,
    window_composer_position,
    needed_composers,
    composer_storage_index,
):
    f32, bf16 = jnp.float32, jnp.bfloat16
    dp_count = lax.axis_size("dp")
    fsdp_count = lax.axis_size("fsdp")
    group_index = lax.axis_index("dp")
    member_index = lax.axis_index("fsdp")
    tok_rows, width = tokens.shape
    value_cols = frozen_value_matrix.shape[1]
    rank = adapter_down_maps.shape[1]
    each_owner_rows = adapter_down_maps.shape[0]
    down_cols = adapter_down_maps.shape[2]
    up_cols = adapter_up_maps.shape[2]
    list_len = needed_composers.shape[1]
    windows = tok_rows // WIN

    part_cols = value_cols // dp_count
    w_part = lax.dynamic_slice_in_dim(
        frozen_value_matrix, group_index * part_cols, part_cols, axis=1
    )
    w_part_full = lax.all_gather(w_part, "fsdp", axis=0, tiled=True)
    up_x = [(i, (i + 2) % dp_count) for i in range(dp_count)]
    down_x = [(i, (i - 2) % dp_count) for i in range(dp_count)]
    from_left = lax.ppermute(w_part_full, "dp", up_x)
    from_right = lax.ppermute(w_part_full, "dp", down_x)
    half_part = part_cols // 2
    far_a = lax.ppermute(from_left[:, :half_part], "dp", up_x)
    far_b = lax.ppermute(from_right[:, half_part:], "dp", down_x)
    far = jnp.concatenate([far_a, far_b], axis=1)
    same_parity = [w_part_full, from_left, far, from_right]
    w_own = jnp.concatenate(same_parity, axis=1)
    w_partner = lax.ppermute(w_own, "dp", [(i, i ^ 1) for i in range(dp_count)])
    out_own = jnp.dot(tokens, w_own, preferred_element_type=f32)
    out_partner = jnp.dot(tokens, w_partner, preferred_element_type=f32)
    held = jnp.concatenate([out_own, out_partner], axis=1).reshape(tok_rows, dp_count, part_cols)
    part_ids = jnp.arange(dp_count, dtype=jnp.int32)
    partner_index = group_index ^ 1
    same = (part_ids % 2) == (group_index % 2)
    where_held = jnp.where(
        same,
        ((group_index - part_ids) % dp_count) // 2,
        dp_count // 2 + ((partner_index - part_ids) % dp_count) // 2,
    )
    frozen_rows = jnp.take(held, where_held, axis=1).reshape(tok_rows, value_cols)

    list_slot = jnp.take(composer_storage_index, needed_composers, axis=0)
    list_owner = list_slot // each_owner_rows
    list_local = list_slot % each_owner_rows
    owned_here = list_owner == group_index
    locally_owned_slots = jnp.sum(jnp.where(owned_here, list_local, 0), axis=1)
    owned_any = jnp.any(owned_here, axis=1)
    send = jnp.concatenate(
        [
            jnp.take(adapter_down_maps, locally_owned_slots, axis=0),
            jnp.take(adapter_up_maps, locally_owned_slots, axis=0),
        ],
        axis=2,
    )
    send = jnp.where(owned_any[:, None, None], send, jnp.zeros((), send.dtype))
    got = lax.all_to_all(send, "dp", split_axis=0, concat_axis=0, tiled=True)
    my_owner = lax.dynamic_index_in_dim(list_owner, group_index, 0, keepdims=False)
    slab = jnp.take(got, my_owner, axis=0)
    shares = lax.all_gather(slab, "fsdp", axis=0, tiled=False)
    full_down = shares[..., :down_cols].transpose(1, 2, 0, 3).reshape(list_len, rank, width)
    full_up = shares[..., down_cols:].transpose(1, 2, 0, 3).reshape(list_len, rank, value_cols)

    group_picks = window_composer_position[0]
    my_picks = lax.dynamic_slice_in_dim(group_picks, member_index * windows, windows, 0)
    slot_range = jnp.arange(list_len, dtype=jnp.int32)
    token_hot = jnp.broadcast_to(
        my_picks[:, None, None] == slot_range[None, None, :], (windows, WIN, list_len)
    ).reshape(tok_rows, list_len)
    hot_f = token_hot.astype(f32)

    down_flat = full_down.reshape(list_len * rank, width)
    up_flat = full_up.reshape(list_len * rank, value_cols)
    low_all = lax.dot_general(
        tokens, down_flat, (((1,), (1,)), ((), ())), preferred_element_type=f32
    ).reshape(tok_rows, list_len, rank)
    low = jnp.sum(low_all * hot_f[:, :, None], axis=1).astype(bf16)
    hot_h = token_hot.astype(bf16)
    masked_low = (hot_h[:, :, None] * low[:, None, :]).reshape(tok_rows, list_len * rank)
    adapter_change = jnp.dot(masked_low, up_flat, preferred_element_type=f32)
    value = (frozen_rows + ADAPTER_SCALE * adapter_change).astype(bf16)

    back_all = lax.dot_general(
        value_output_gradient, up_flat, (((1,), (1,)), ((), ())), preferred_element_type=f32
    ).reshape(tok_rows, list_len, rank)
    back = (ADAPTER_SCALE * jnp.sum(back_all * hot_f[:, :, None], axis=1)).astype(bf16)
    masked_back = (hot_h[:, :, None] * back[:, None, :]).reshape(tok_rows, list_len * rank)
    scaled_masked_low = masked_low * jnp.asarray(ADAPTER_SCALE, bf16)

    contract = (((0,), (0,)), ((), ()))
    part_down = lax.dot_general(masked_back, tokens, contract, preferred_element_type=f32)
    part_up = lax.dot_general(
        scaled_masked_low, value_output_gradient, contract, preferred_element_type=f32
    )
    rows = list_len * rank
    part_down = part_down.reshape(rows, fsdp_count, down_cols).transpose(1, 0, 2)
    part_up = part_up.reshape(rows, fsdp_count, up_cols).transpose(1, 0, 2)
    summed = lax.psum_scatter(
        jnp.concatenate([part_down, part_up], axis=2), "fsdp", scatter_dimension=0, tiled=True
    )[0]

    owner_range = jnp.arange(dp_count, dtype=jnp.int32)
    to_owner = my_owner[None, :] == owner_range[:, None]
    pick_index = jnp.sum(jnp.where(to_owner, slot_range[None, :], 0), axis=1)
    owner_has = jnp.any(to_owner, axis=1)
    send_grad = jnp.take(summed.reshape(list_len, rank, down_cols + up_cols), pick_index, axis=0)
    back_grad = lax.all_to_all(send_grad, "dp", split_axis=0, concat_axis=0, tiled=True)
    land = jnp.where(owned_any, locally_owned_slots, 0)
    arrived = jnp.where(owned_any[:, None, None], back_grad, 0.0)
    grad_down = jnp.zeros((each_owner_rows, rank, down_cols), f32).at[land].add(
        arrived[:, :, :down_cols]
    )
    grad_up = jnp.zeros((each_owner_rows, rank, up_cols), f32).at[land].add(
        arrived[:, :, down_cols:]
    )
    return (value, grad_down, grad_up)


def solution(mesh):
    return jax.shard_map(
        body,
        mesh=mesh,
        in_specs=(
            P(("dp", "fsdp"), None),
            P("fsdp", None),
            P("dp", None, "fsdp"),
            P("dp", None, "fsdp"),
            P(("dp", "fsdp"), None),
            P("dp", None),
            P(),
            P(),
        ),
        out_specs=(P(("dp", "fsdp"), None), P("dp", None, "fsdp"), P("dp", None, "fsdp")),
        check_vma=False,
    )
```
